128 devices in a mesh: runs: 32 (over x, z, y_hi), chan: 4 (over y_lo, core).
Axes of the slice: x: 4, y: 4 (y_hi: 2, y_lo: 2; y = y_hi * 2 + y_lo), z: 4, core: 2. Of those that a mesh axis runs over, the one named last changes fastest.
Arguments:
- slices: bfloat16 [256, 512, 8192], P('runs', None, 'chan'), may hold values from -6 to 6
- spectra: bfloat16 [2, 48, 8192], P(None, None, 'chan'), may hold values from -0.0625 to 0.0625
- loadings: float32 [256, 48], replicated, may hold values from 0.5 to 2
- mixing: float32 [2, 48, 48], replicated, may hold values from -1 to 3.5
- halves: int32 [256], replicated, may hold values from 0 to 1, as said below
- partner: int32 [256], replicated, may hold values from 0 to 255, as said below
Outputs:
- new_spectra: float32 [2, 48, 8192], P(None, None, 'chan')
- held_residual: float32 [256, 48, 8192], P('runs', None, 'chan')
The draws below stay inside these ranges and needn't reach their ends.
Inputs may be any that keep to these rules, and one draw needn't show every extreme that they name: `halves`: exactly half of the 256 runs are in each half. partner pairs every run with a run of the other half, and the partner of a run's partner is the run itself.
All inputs are finite; a program needn't handle non-finite values.
Results may differ from the reference program's by a relative error of at most 0.0045.
Values may be sent and summed in bfloat16 or wider, within the bound.
No kernel may reach another device: no remote copies, remote signals or barrier semaphores. Data moves between devices by JAX's collectives and lax.ppermute only.
A program may use at most 64 MiB of HBM per device.

```python
import math
import jax
import jax.numpy as jnp
from jax import lax

R = 48
TIMES = 512
J = 8192
NS_STEPS = 10
RUNS = 256


def pairing(key):
    order = jax.random.permutation(jax.random.fold_in(key, 11), RUNS).astype(jnp.int32)
    middle = RUNS // 2
    places = jnp.arange(RUNS, dtype=jnp.int32)
    labels = jnp.zeros((RUNS,), jnp.int32).at[order].set((places >= middle).astype(jnp.int32))
    mates = jnp.zeros((RUNS,), jnp.int32).at[order].set(jnp.roll(order, middle))
    return (labels, mates)


def draw_halves(key, part):
    return pairing(key)[0]


def draw_partner(key, part):
    return pairing(key)[1]


def draw_slices(key, part):
    first = jax.random.fold_in(jax.random.fold_in(key, 7), 0)
    values = jnp.clip(jax.random.normal(first, (RUNS, TIMES, J), jnp.float32), -6.0, 6.0)
    return values.astype(jnp.bfloat16)


def draw_mixing(key, part):
    first, second = jax.random.split(jax.random.fold_in(key, 5))
    diagonal = jax.random.uniform(first, (2, R), jnp.float32, 2.0, 3.0)
    spread = jnp.clip(0.12 * jax.random.normal(second, (2, R, R), jnp.float32), -0.45, 0.45)
    return spread + diagonal[:, :, None] * jnp.eye(R, dtype=jnp.float32)[None]


def shard_levels(own_key, dims, pieces, smallest, high):
    gain = 1.0
    for dim, shards_of in pieces:
        draws = jax.random.uniform(jax.random.fold_in(jax.random.fold_in(own_key, 6), dim), (shards_of,), jnp.float32, smallest / len(pieces), high / len(pieces))
        gain = gain * jnp.repeat(jnp.exp(draws), dims[dim] // shards_of).reshape((-1,) + (1,) * (len(dims) - 1 - dim))
    return gain


def noise(rng, dims, width, bound, cuts=(), held_as=jnp.bfloat16):
    result = jax.random.normal(rng, dims, jnp.float32) * width
    if len(cuts) > 0:
        result = shard_levels(rng, dims, cuts, -0.22, 0.18) * result
    return jnp.clip(result, min=-bound, max=bound).astype(held_as)


def setup_inputs(seed: int = 0) -> dict:
    key_list = jax.random.split(jax.random.key(seed), 7)
    slices = draw_slices(jax.random.fold_in(key_list[6], 71), 0)
    spectra = noise(key_list[1], (2, R, J), J ** -0.5, 0.0625, ((2, 4),))
    loadings = jnp.clip(jnp.exp(jax.random.uniform(key_list[2], (RUNS, R), jnp.float32, math.log(0.5), math.log(2.0))), 0.5, 2.0)
    mixing = draw_mixing(jax.random.fold_in(key_list[6], 71), 0)
    halves = draw_halves(jax.random.fold_in(key_list[6], 71), 0)
    partner = draw_partner(jax.random.fold_in(key_list[6], 71), 0)
    return dict(slices=slices, spectra=spectra, loadings=loadings, mixing=mixing, halves=halves, partner=partner)


def polar_scale(gram):
    eye_rank = jnp.eye(gram.shape[-1], dtype=gram.dtype)
    start = eye_rank / jnp.sqrt(jnp.trace(gram) + 1e-06)

    def advance(step, factor):
        inner = jnp.dot(jnp.dot(factor.T, gram, precision=lax.Precision.HIGHEST), factor, precision=lax.Precision.HIGHEST)
        return 0.5 * jnp.dot(factor, 3.0 * eye_rank - inner, precision=lax.Precision.HIGHEST)
    return lax.fori_loop(0, NS_STEPS, advance, start)

def project(slice_run, rows_low, mixed):
    basis = jnp.dot(rows_low.astype(jnp.float32), slice_run.T.astype(jnp.float32), preferred_element_type=jnp.float32)
    scaled = jnp.dot(mixed, basis, precision=lax.Precision.HIGHEST)
    gram = jnp.dot(scaled, scaled.T, precision=lax.Precision.HIGHEST)
    factor = polar_scale(gram)
    rotated = jnp.dot(factor.T, scaled, precision=lax.Precision.HIGHEST).astype(jnp.bfloat16)
    return jnp.dot(rotated.astype(jnp.float32), slice_run.astype(jnp.float32), preferred_element_type=jnp.float32)

def solve_one(lower, target):
    return jax.scipy.linalg.cho_solve((lower, True), target)

def reference(slices, spectra, loadings, mixing, halves, partner):

    def fit_step(total, item):
        slice_run, half_id, loading = item
        mixed = mixing[half_id] * loading[None, :]
        projected = project(slice_run, spectra[half_id], mixed)
        term = jnp.dot(mixed.T, projected, precision=lax.Precision.HIGHEST)
        member_one = (jnp.arange(2, dtype=jnp.int32) == half_id).astype(total.dtype)
        return (total + member_one[:, None, None] * term[None], None)
    empty = jnp.zeros((2, R, J), jnp.float32)
    moments, _ = lax.scan(fit_step, empty, (slices, halves, loadings))
    member = (halves[:, None] == jnp.arange(2, dtype=jnp.int32)[None, :]).astype(loadings.dtype)
    cross = jnp.einsum('kh,kr,ks->hrs', member, loadings, loadings, precision=lax.Precision.HIGHEST)
    inner_mix = jnp.einsum('hsr,hst->hrt', mixing, mixing, precision=lax.Precision.HIGHEST)
    system = inner_mix * cross
    lower = jnp.linalg.cholesky(system)
    new_spectra = jax.vmap(solve_one)(lower, moments)

    def held_step(item):
        slice_run, half_id, mate = item
        other = 1 - half_id
        mixed = mixing[other] * loadings[mate][None, :]
        fitted = new_spectra[other]
        projected = project(slice_run, fitted.astype(jnp.bfloat16), mixed)
        return projected - jnp.dot(mixed, fitted, precision=lax.Precision.HIGHEST)
    held_residual = lax.map(held_step, (slices, halves, partner))
    return (new_spectra, held_residual)
```

```python
import jax
import jax.numpy as jnp
from jax import lax
from jax.sharding import PartitionSpec as P

NS_STEPS = 10


def polar_scale(gram):
    eye_rank = jnp.eye(gram.shape[-1], dtype=jnp.float32)
    traces = jnp.trace(gram, axis1=1, axis2=2)
    start = eye_rank[None] / jnp.sqrt(traces + 1e-06)[:, None, None]

    def advance(step, factor):
        left = jnp.einsum("nrs,nrt->nst", factor, gram, precision=lax.Precision.HIGHEST)
        inner = jnp.einsum("nst,ntu->nsu", left, factor, precision=lax.Precision.HIGHEST)
        return 0.5 * jnp.einsum(
            "nrs,nsu->nru", factor, 3.0 * eye_rank[None] - inner, precision=lax.Precision.HIGHEST
        )

    return lax.fori_loop(0, NS_STEPS, advance, start)


def step_bits(size, order):
    bits = [b for b in order if b < size]
    if sorted(bits) != [1 << i for i in range(size.bit_length() - 1)]:
        bits = [1 << i for i in range(size.bit_length() - 1)]
    return bits


def xor_pairs(size, bit):
    return [(i, i ^ bit) for i in range(size)]


def halving_scatter(x, axis, size, bits, dim):
    idx = lax.axis_index(axis)
    for bit in bits:
        hi = (idx & bit) != 0
        half = x.shape[dim] // 2
        low = lax.slice_in_dim(x, 0, half, axis=dim)
        high = lax.slice_in_dim(x, half, 2 * half, axis=dim)
        send = jnp.where(hi, low, high)
        keep = jnp.where(hi, high, low)
        x = keep + lax.ppermute(send, axis, xor_pairs(size, bit))
    return x


def doubling_gather(x, axis, size, bits, dim):
    idx = lax.axis_index(axis)
    for bit in reversed(bits):
        hi = (idx & bit) != 0
        got = lax.ppermute(x, axis, xor_pairs(size, bit))
        x = jnp.where(hi, jnp.concatenate([got, x], dim), jnp.concatenate([x, got], dim))
    return x


def block_index(axis, bits):
    idx = lax.axis_index(axis)
    block = jnp.int32(0)
    for bit in bits:
        block = block * 2 + ((idx & bit) != 0).astype(jnp.int32)
    return block


def project(slices, rows_low, mixed, chan_size, chan_bits):
    run_count = slices.shape[0]
    partial_basis = jnp.einsum("nrj,nij->nri", rows_low, slices, preferred_element_type=jnp.float32)
    basis = halving_scatter(partial_basis, "chan", chan_size, chan_bits, 0)
    part = basis.shape[0]
    first = block_index("chan", chan_bits) * part
    mixed_part = lax.dynamic_slice_in_dim(mixed, first, part, axis=0)
    scaled = jnp.einsum("nrs,nsi->nri", mixed_part, basis, precision=lax.Precision.HIGHEST)
    gram = jnp.einsum("nri,nsi->nrs", scaled, scaled, precision=lax.Precision.HIGHEST)
    factor = polar_scale(gram)
    rotated = jnp.einsum("nrs,nri->nsi", factor, scaled, precision=lax.Precision.HIGHEST).astype(
        jnp.bfloat16
    )
    rotated = doubling_gather(rotated, "chan", chan_size, chan_bits, 0)
    del run_count
    return jnp.einsum("nsi,nij->nsj", rotated, slices, preferred_element_type=jnp.float32)


def solve_one(lower, target):
    return jax.scipy.linalg.cho_solve((lower, True), target)


def make_body(runs_size, chan_size):
    runs_bits = step_bits(runs_size, (8, 2, 1, 16, 4))
    chan_bits = step_bits(chan_size, (1, 2))

    def body(slices, spectra, loadings, mixing, halves, partner):
        run_count = slices.shape[0]
        total_runs = loadings.shape[0]
        first_run = lax.axis_index("runs") * run_count
        mine = first_run + jnp.arange(run_count, dtype=jnp.int32)
        all_runs = jnp.arange(total_runs, dtype=jnp.int32)
        matches = all_runs[None, :] == mine[:, None]
        my_halves = jnp.sum(jnp.where(matches, halves[None, :], 0), axis=1)
        my_mates = jnp.sum(jnp.where(matches, partner[None, :], 0), axis=1)
        my_loads = jnp.dot(matches.astype(jnp.float32), loadings, precision=lax.Precision.HIGHEST)
        mate_match = (all_runs[None, :] == my_mates[:, None]).astype(jnp.float32)
        mate_loads = jnp.dot(mate_match, loadings, precision=lax.Precision.HIGHEST)
        first_half = (my_halves == 0)[:, None, None]
        own_rows = jnp.where(first_half, spectra[0][None], spectra[1][None])
        own_mix = jnp.where(first_half, mixing[0][None], mixing[1][None]) * my_loads[:, None, :]
        projected = project(slices, own_rows, own_mix, chan_size, chan_bits)
        terms = jnp.einsum("nsr,nsj->nrj", own_mix, projected, precision=lax.Precision.HIGHEST)
        mine_member = (my_halves[:, None] == jnp.arange(2, dtype=jnp.int32)[None, :]).astype(
            jnp.float32
        )
        partial_moments = jnp.einsum(
            "nh,nrj->hrj", mine_member, terms, precision=lax.Precision.HIGHEST
        )
        member = (halves[:, None] == jnp.arange(2, dtype=jnp.int32)[None, :]).astype(jnp.float32)
        cross = jnp.einsum("kh,kr,ks->hrs", member, loadings, loadings, precision=lax.Precision.HIGHEST)
        inner_mix = jnp.einsum("hsr,hst->hrt", mixing, mixing, precision=lax.Precision.HIGHEST)
        system = inner_mix * cross
        lower = jnp.linalg.cholesky(system)
        moments_part = halving_scatter(partial_moments, "runs", runs_size, runs_bits, 2)
        spectra_part = jax.vmap(solve_one)(lower, moments_part)
        new_spectra = doubling_gather(spectra_part, "runs", runs_size, runs_bits, 2)
        held_rows = jnp.where(first_half, new_spectra[1][None], new_spectra[0][None])
        held_mix = jnp.where(first_half, mixing[1][None], mixing[0][None]) * mate_loads[:, None, :]
        held_projected = project(
            slices, held_rows.astype(jnp.bfloat16), held_mix, chan_size, chan_bits
        )
        model_part = jnp.einsum(
            "nrs,nsj->nrj", held_mix, held_rows, precision=lax.Precision.HIGHEST
        )
        return (new_spectra, held_projected - model_part)

    return body


def solution(mesh):
    placed = (P("runs", None, "chan"), P(None, None, "chan"), P(), P(), P(), P())
    return jax.shard_map(
        make_body(mesh.shape["runs"], mesh.shape["chan"]),
        mesh=mesh,
        in_specs=placed,
        out_specs=(P(None, None, "chan"), P("runs", None, "chan")),
        check_vma=False,
    )
```

```python
import jax
import jax.numpy as jnp
from jax import lax
from jax.sharding import PartitionSpec as P

NS_STEPS = 10


def polar_scale(gram):
    eye_rank = jnp.eye(gram.shape[-1], dtype=jnp.float32)
    traces = jnp.trace(gram, axis1=1, axis2=2)
    start = eye_rank[None] / jnp.sqrt(traces + 1e-06)[:, None, None]

    def advance(step, factor):
        left = jnp.einsum("nrs,nrt->nst", factor, gram, precision=lax.Precision.HIGHEST)
        inner = jnp.einsum("nst,ntu->nsu", left, factor, precision=lax.Precision.HIGHEST)
        return 0.5 * jnp.einsum(
            "nrs,nsu->nru", factor, 3.0 * eye_rank[None] - inner, precision=lax.Precision.HIGHEST
        )

    return lax.fori_loop(0, NS_STEPS, advance, start)


def step_bits(size, order):
    bits = [b for b in order if b < size]
    if sorted(bits) != [1 << i for i in range(size.bit_length() - 1)]:
        bits = [1 << i for i in range(size.bit_length() - 1)]
    return bits


def xor_pairs(size, bit):
    return [(i, i ^ bit) for i in range(size)]


def halving_scatter(x, axis, size, bits, dim):
    idx = lax.axis_index(axis)
    for bit in bits:
        hi = (idx & bit) != 0
        half = x.shape[dim] // 2
        low = lax.slice_in_dim(x, 0, half, axis=dim)
        high = lax.slice_in_dim(x, half, 2 * half, axis=dim)
        send = jnp.where(hi, low, high)
        keep = jnp.where(hi, high, low)
        x = keep + lax.ppermute(send, axis, xor_pairs(size, bit))
    return x


def doubling_gather(x, axis, size, bits, dim):
    idx = lax.axis_index(axis)
    for bit in reversed(bits):
        hi = (idx & bit) != 0
        got = lax.ppermute(x, axis, xor_pairs(size, bit))
        x = jnp.where(hi, jnp.concatenate([got, x], dim), jnp.concatenate([x, got], dim))
    return x


def block_index(axis, bits):
    idx = lax.axis_index(axis)
    block = jnp.int32(0)
    for bit in bits:
        block = block * 2 + ((idx & bit) != 0).astype(jnp.int32)
    return block


def project(slices, rows_low, mixed, chan_size, chan_bits):
    run_count = slices.shape[0]
    partial_basis = jnp.einsum("nrj,nij->nri", rows_low, slices, preferred_element_type=jnp.float32)
    basis = halving_scatter(partial_basis, "chan", chan_size, chan_bits, 0)
    part = basis.shape[0]
    first = block_index("chan", chan_bits) * part
    mixed_part = lax.dynamic_slice_in_dim(mixed, first, part, axis=0)
    scaled = jnp.einsum("nrs,nsi->nri", mixed_part, basis, precision=lax.Precision.HIGHEST)
    gram = jnp.einsum("nri,nsi->nrs", scaled, scaled, precision=lax.Precision.HIGHEST)
    factor = polar_scale(gram)
    rotated = jnp.einsum("nrs,nri->nsi", factor, scaled, precision=lax.Precision.HIGHEST).astype(
        jnp.bfloat16
    )
    rotated = doubling_gather(rotated, "chan", chan_size, chan_bits, 0)
    del run_count
    return jnp.einsum("nsi,nij->nsj", rotated, slices, preferred_element_type=jnp.float32)


def lower_inverse(system):
    lower = jnp.linalg.cholesky(system)
    eye_rank = jnp.broadcast_to(jnp.eye(system.shape[-1], dtype=system.dtype), system.shape)
    return lax.linalg.triangular_solve(lower, eye_rank, left_side=True, lower=True)


def apply_inverse(inverse, target):
    inner = jnp.einsum("hrs,hsj->hrj", inverse, target, precision=lax.Precision.HIGHEST)
    return jnp.einsum("hsr,hsj->hrj", inverse, inner, precision=lax.Precision.HIGHEST)


def make_body(runs_size, chan_size):
    runs_bits = step_bits(runs_size, (8, 2, 1, 16, 4))
    chan_bits = step_bits(chan_size, (1, 2))

    def body(slices, spectra, loadings, mixing, halves, partner):
        run_count = slices.shape[0]
        total_runs = loadings.shape[0]
        first_run = lax.axis_index("runs") * run_count
        mine = first_run + jnp.arange(run_count, dtype=jnp.int32)
        all_runs = jnp.arange(total_runs, dtype=jnp.int32)
        matches = all_runs[None, :] == mine[:, None]
        my_halves = jnp.sum(jnp.where(matches, halves[None, :], 0), axis=1)
        my_mates = jnp.sum(jnp.where(matches, partner[None, :], 0), axis=1)
        my_loads = jnp.dot(matches.astype(jnp.float32), loadings, precision=lax.Precision.HIGHEST)
        mate_match = (all_runs[None, :] == my_mates[:, None]).astype(jnp.float32)
        mate_loads = jnp.dot(mate_match, loadings, precision=lax.Precision.HIGHEST)
        first_half = (my_halves == 0)[:, None, None]
        own_rows = jnp.where(first_half, spectra[0][None], spectra[1][None])
        own_mix = jnp.where(first_half, mixing[0][None], mixing[1][None]) * my_loads[:, None, :]
        projected = project(slices, own_rows, own_mix, chan_size, chan_bits)
        terms = jnp.einsum("nsr,nsj->nrj", own_mix, projected, precision=lax.Precision.HIGHEST)
        mine_member = (my_halves[:, None] == jnp.arange(2, dtype=jnp.int32)[None, :]).astype(
            jnp.float32
        )
        partial_moments = jnp.einsum(
            "nh,nrj->hrj", mine_member, terms, precision=lax.Precision.HIGHEST
        )
        member = (halves[:, None] == jnp.arange(2, dtype=jnp.int32)[None, :]).astype(jnp.float32)
        cross = jnp.einsum("kh,kr,ks->hrs", member, loadings, loadings, precision=lax.Precision.HIGHEST)
        inner_mix = jnp.einsum("hsr,hst->hrt", mixing, mixing, precision=lax.Precision.HIGHEST)
        system = inner_mix * cross
        inverse = lower_inverse(system)
        moments_part = halving_scatter(partial_moments, "runs", runs_size, runs_bits, 2)
        spectra_part = apply_inverse(inverse, moments_part)
        new_spectra = doubling_gather(spectra_part, "runs", runs_size, runs_bits, 2)
        held_rows = jnp.where(first_half, new_spectra[1][None], new_spectra[0][None])
        held_mix = jnp.where(first_half, mixing[1][None], mixing[0][None]) * mate_loads[:, None, :]
        held_projected = project(
            slices, held_rows.astype(jnp.bfloat16), held_mix, chan_size, chan_bits
        )
        model_part = jnp.einsum(
            "nrs,nsj->nrj", held_mix, held_rows, precision=lax.Precision.HIGHEST
        )
        return (new_spectra, held_projected - model_part)

    return body


def solution(mesh):
    placed = (P("runs", None, "chan"), P(None, None, "chan"), P(), P(), P(), P())
    return jax.shard_map(
        make_body(mesh.shape["runs"], mesh.shape["chan"]),
        mesh=mesh,
        in_specs=placed,
        out_specs=(P(None, None, "chan"), P("runs", None, "chan")),
        check_vma=False,
    )
```

```python
import jax
import jax.numpy as jnp
from jax import lax
from jax.sharding import PartitionSpec as P

NS_STEPS = 10


def polar_scale(gram):
    eye_rank = jnp.eye(gram.shape[-1], dtype=jnp.float32)
    traces = jnp.trace(gram, axis1=1, axis2=2)
    start = eye_rank[None] / jnp.sqrt(traces + 1e-06)[:, None, None]

    def advance(step, factor):
        left = jnp.einsum("nrs,nrt->nst", factor, gram, precision=lax.Precision.HIGHEST)
        inner = jnp.einsum("nst,ntu->nsu", left, factor, precision=lax.Precision.HIGHEST)
        return 0.5 * jnp.einsum(
            "nrs,nsu->nru", factor, 3.0 * eye_rank[None] - inner, precision=lax.Precision.HIGHEST
        )

    return lax.fori_loop(0, NS_STEPS, advance, start)


def step_bits(size, order):
    bits = [b for b in order if b < size]
    if sorted(bits) != [1 << i for i in range(size.bit_length() - 1)]:
        bits = [1 << i for i in range(size.bit_length() - 1)]
    return bits


def xor_pairs(size, bit):
    return [(i, i ^ bit) for i in range(size)]


def halving_scatter(x, axis, size, bits, dim):
    idx = lax.axis_index(axis)
    for bit in bits:
        hi = (idx & bit) != 0
        half = x.shape[dim] // 2
        low = lax.slice_in_dim(x, 0, half, axis=dim)
        high = lax.slice_in_dim(x, half, 2 * half, axis=dim)
        send = jnp.where(hi, low, high)
        keep = jnp.where(hi, high, low)
        x = keep + lax.ppermute(send, axis, xor_pairs(size, bit))
    return x


def doubling_gather(x, axis, size, bits, dim):
    idx = lax.axis_index(axis)
    for bit in reversed(bits):
        hi = (idx & bit) != 0
        got = lax.ppermute(x, axis, xor_pairs(size, bit))
        x = jnp.where(hi, jnp.concatenate([got, x], dim), jnp.concatenate([x, got], dim))
    return x


def digit(idx, bits):
    value = jnp.int32(0)
    for j, bit in enumerate(bits):
        value = value + ((idx & bit) != 0).astype(jnp.int32) * (1 << j)
    return value


def partner_mask(bits, offset):
    return sum(bit for j, bit in enumerate(bits) if (offset >> j) & 1)


def radix_scatter(x, axis, size, groups, dim):
    idx = lax.axis_index(axis)
    for bits in groups:
        radix = 1 << len(bits)
        width = x.shape[dim] // radix
        mine = digit(idx, bits)
        acc = lax.dynamic_slice_in_dim(x, mine * width, width, axis=dim)
        for offset in range(1, radix):
            mask = partner_mask(bits, offset)
            send = lax.dynamic_slice_in_dim(x, (mine ^ offset) * width, width, axis=dim)
            acc = acc + lax.ppermute(send, axis, xor_pairs(size, mask))
        x = acc
    return x


def radix_gather(x, axis, size, groups, dim):
    idx = lax.axis_index(axis)
    for bits in reversed(groups):
        radix = 1 << len(bits)
        width = x.shape[dim]
        mine = digit(idx, bits)
        shape = list(x.shape)
        shape[dim] = width * radix
        out = lax.dynamic_update_slice_in_dim(jnp.zeros(shape, x.dtype), x, mine * width, axis=dim)
        for offset in range(1, radix):
            mask = partner_mask(bits, offset)
            got = lax.ppermute(x, axis, xor_pairs(size, mask))
            out = lax.dynamic_update_slice_in_dim(out, got, (mine ^ offset) * width, axis=dim)
        x = out
    return x


def radix_groups(size, groups):
    flat = sorted(bit for bits in groups for bit in bits)
    if flat != [1 << i for i in range(size.bit_length() - 1)]:
        return [(1 << i,) for i in range(size.bit_length() - 1)]
    return groups


def block_index(axis, bits):
    idx = lax.axis_index(axis)
    block = jnp.int32(0)
    for bit in bits:
        block = block * 2 + ((idx & bit) != 0).astype(jnp.int32)
    return block


def project(slices, rows_low, mixed, chan_size, chan_bits):
    run_count = slices.shape[0]
    partial_basis = jnp.einsum("nrj,nij->nri", rows_low, slices, preferred_element_type=jnp.float32)
    basis = halving_scatter(partial_basis, "chan", chan_size, chan_bits, 0)
    part = basis.shape[0]
    first = block_index("chan", chan_bits) * part
    mixed_part = lax.dynamic_slice_in_dim(mixed, first, part, axis=0)
    scaled = jnp.einsum("nrs,nsi->nri", mixed_part, basis, precision=lax.Precision.HIGHEST)
    gram = jnp.einsum("nri,nsi->nrs", scaled, scaled, precision=lax.Precision.HIGHEST)
    factor = polar_scale(gram)
    rotated = jnp.einsum("nrs,nri->nsi", factor, scaled, precision=lax.Precision.HIGHEST).astype(
        jnp.bfloat16
    )
    rotated = doubling_gather(rotated, "chan", chan_size, chan_bits, 0)
    del run_count
    return jnp.einsum("nsi,nij->nsj", rotated, slices, preferred_element_type=jnp.float32)


def lower_inverse(system):
    lower = jnp.linalg.cholesky(system)
    eye_rank = jnp.broadcast_to(jnp.eye(system.shape[-1], dtype=system.dtype), system.shape)
    return lax.linalg.triangular_solve(lower, eye_rank, left_side=True, lower=True)


def apply_inverse(inverse, target):
    inner = jnp.einsum("hrs,hsj->hrj", inverse, target, precision=lax.Precision.HIGHEST)
    return jnp.einsum("hsr,hsj->hrj", inverse, inner, precision=lax.Precision.HIGHEST)


def make_body(runs_size, chan_size):
    runs_groups = radix_groups(runs_size, [(8, 16), (2, 4), (1,)])
    chan_bits = step_bits(chan_size, (1, 2))

    def body(slices, spectra, loadings, mixing, halves, partner):
        run_count = slices.shape[0]
        total_runs = loadings.shape[0]
        first_run = lax.axis_index("runs") * run_count
        mine = first_run + jnp.arange(run_count, dtype=jnp.int32)
        all_runs = jnp.arange(total_runs, dtype=jnp.int32)
        matches = all_runs[None, :] == mine[:, None]
        my_halves = jnp.sum(jnp.where(matches, halves[None, :], 0), axis=1)
        my_mates = jnp.sum(jnp.where(matches, partner[None, :], 0), axis=1)
        my_loads = jnp.dot(matches.astype(jnp.float32), loadings, precision=lax.Precision.HIGHEST)
        mate_match = (all_runs[None, :] == my_mates[:, None]).astype(jnp.float32)
        mate_loads = jnp.dot(mate_match, loadings, precision=lax.Precision.HIGHEST)
        first_half = (my_halves == 0)[:, None, None]
        own_rows = jnp.where(first_half, spectra[0][None], spectra[1][None])
        own_mix = jnp.where(first_half, mixing[0][None], mixing[1][None]) * my_loads[:, None, :]
        projected = project(slices, own_rows, own_mix, chan_size, chan_bits)
        terms = jnp.einsum("nsr,nsj->nrj", own_mix, projected, precision=lax.Precision.HIGHEST)
        mine_member = (my_halves[:, None] == jnp.arange(2, dtype=jnp.int32)[None, :]).astype(
            jnp.float32
        )
        partial_moments = jnp.einsum(
            "nh,nrj->hrj", mine_member, terms, precision=lax.Precision.HIGHEST
        )
        member = (halves[:, None] == jnp.arange(2, dtype=jnp.int32)[None, :]).astype(jnp.float32)
        cross = jnp.einsum("kh,kr,ks->hrs", member, loadings, loadings, precision=lax.Precision.HIGHEST)
        inner_mix = jnp.einsum("hsr,hst->hrt", mixing, mixing, precision=lax.Precision.HIGHEST)
        system = inner_mix * cross
        inverse = lower_inverse(system)
        moments_part = radix_scatter(partial_moments, "runs", runs_size, runs_groups, 2)
        spectra_part = apply_inverse(inverse, moments_part)
        new_spectra = radix_gather(spectra_part, "runs", runs_size, runs_groups, 2)
        held_rows = jnp.where(first_half, new_spectra[1][None], new_spectra[0][None])
        held_mix = jnp.where(first_half, mixing[1][None], mixing[0][None]) * mate_loads[:, None, :]
        held_projected = project(
            slices, held_rows.astype(jnp.bfloat16), held_mix, chan_size, chan_bits
        )
        model_part = jnp.einsum(
            "nrs,nsj->nrj", held_mix, held_rows, precision=lax.Precision.HIGHEST
        )
        return (new_spectra, held_projected - model_part)

    return body


def solution(mesh):
    placed = (P("runs", None, "chan"), P(None, None, "chan"), P(), P(), P(), P())
    return jax.shard_map(
        make_body(mesh.shape["runs"], mesh.shape["chan"]),
        mesh=mesh,
        in_specs=placed,
        out_specs=(P(None, None, "chan"), P("runs", None, "chan")),
        check_vma=False,
    )
```

```python
import jax
import jax.numpy as jnp
from jax import lax
from jax.sharding import PartitionSpec as P

NS_STEPS = 10


def polar_scale(gram):
    eye_rank = jnp.eye(gram.shape[-1], dtype=jnp.float32)
    traces = jnp.trace(gram, axis1=1, axis2=2)
    start = eye_rank[None] / jnp.sqrt(traces + 1e-06)[:, None, None]

    def advance(step, factor):
        left = jnp.einsum("nrs,nrt->nst", factor, gram, precision=lax.Precision.HIGHEST)
        inner = jnp.einsum("nst,ntu->nsu", left, factor, precision=lax.Precision.HIGHEST)
        return 0.5 * jnp.einsum(
            "nrs,nsu->nru", factor, 3.0 * eye_rank[None] - inner, precision=lax.Precision.HIGHEST
        )

    return lax.fori_loop(0, NS_STEPS, advance, start)


def step_bits(size, order):
    bits = [b for b in order if b < size]
    if sorted(bits) != [1 << i for i in range(size.bit_length() - 1)]:
        bits = [1 << i for i in range(size.bit_length() - 1)]
    return bits


def xor_pairs(size, bit):
    return [(i, i ^ bit) for i in range(size)]


def halving_scatter(x, axis, size, bits, dim):
    idx = lax.axis_index(axis)
    for bit in bits:
        hi = (idx & bit) != 0
        half = x.shape[dim] // 2
        low = lax.slice_in_dim(x, 0, half, axis=dim)
        high = lax.slice_in_dim(x, half, 2 * half, axis=dim)
        send = jnp.where(hi, low, high)
        keep = jnp.where(hi, high, low)
        got = lax.ppermute(send, axis, xor_pairs(size, bit))
        x = keep + got
    return x


def doubling_gather(x, axis, size, bits, dim):
    idx = lax.axis_index(axis)
    for bit in reversed(bits):
        hi = (idx & bit) != 0
        got = lax.ppermute(x, axis, xor_pairs(size, bit))
        x = jnp.where(hi, jnp.concatenate([got, x], dim), jnp.concatenate([x, got], dim))
    return x


def digit(idx, bits):
    value = jnp.int32(0)
    for j, bit in enumerate(bits):
        value = value + ((idx & bit) != 0).astype(jnp.int32) * (1 << j)
    return value


def partner_mask(bits, offset):
    return sum(bit for j, bit in enumerate(bits) if (offset >> j) & 1)


def radix_scatter(x, axis, size, groups, dim):
    idx = lax.axis_index(axis)
    for bits in groups:
        radix = 1 << len(bits)
        width = x.shape[dim] // radix
        mine = digit(idx, bits)
        acc = lax.dynamic_slice_in_dim(x, mine * width, width, axis=dim)
        for offset in range(1, radix):
            mask = partner_mask(bits, offset)
            send = lax.dynamic_slice_in_dim(x, (mine ^ offset) * width, width, axis=dim)
            got = lax.ppermute(send, axis, xor_pairs(size, mask))
            acc = acc + got
        x = acc
    return x


def radix_gather(x, axis, size, groups, dim):
    idx = lax.axis_index(axis)
    for bits in reversed(groups):
        radix = 1 << len(bits)
        width = x.shape[dim]
        mine = digit(idx, bits)
        shape = list(x.shape)
        shape[dim] = width * radix
        out = lax.dynamic_update_slice_in_dim(jnp.zeros(shape, x.dtype), x, mine * width, axis=dim)
        for offset in range(1, radix):
            mask = partner_mask(bits, offset)
            got = lax.ppermute(x, axis, xor_pairs(size, mask))
            out = lax.dynamic_update_slice_in_dim(out, got, (mine ^ offset) * width, axis=dim)
        x = out
    return x


def radix_groups(size, groups):
    flat = sorted(bit for bits in groups for bit in bits)
    if flat != [1 << i for i in range(size.bit_length() - 1)]:
        return [(1 << i,) for i in range(size.bit_length() - 1)]
    return groups


def block_index(axis, bits):
    idx = lax.axis_index(axis)
    block = jnp.int32(0)
    for bit in bits:
        block = block * 2 + ((idx & bit) != 0).astype(jnp.int32)
    return block


def project_body(slices, rows_low, mixed, chan_size, chan_bits):
    run_count = slices.shape[0]
    partial_basis = jnp.einsum("nrj,nij->nri", rows_low, slices, preferred_element_type=jnp.float32)
    basis = halving_scatter(partial_basis, "chan", chan_size, chan_bits, 0)
    part = basis.shape[0]
    first = block_index("chan", chan_bits) * part
    mixed_part = lax.dynamic_slice_in_dim(mixed, first, part, axis=0)
    scaled = jnp.einsum("nrs,nsi->nri", mixed_part, basis, precision=lax.Precision.HIGHEST)
    gram = jnp.einsum("nri,nsi->nrs", scaled, scaled, precision=lax.Precision.HIGHEST)
    factor = polar_scale(gram)
    rotated = jnp.einsum("nrs,nri->nsi", factor, scaled, precision=lax.Precision.HIGHEST).astype(
        jnp.bfloat16
    )
    rotated = doubling_gather(rotated, "chan", chan_size, chan_bits, 0)
    del run_count
    return jnp.einsum("nsi,nij->nsj", rotated, slices, preferred_element_type=jnp.float32)


def lower_inverse(system):
    lower = jnp.linalg.cholesky(system)
    eye_rank = jnp.broadcast_to(jnp.eye(system.shape[-1], dtype=system.dtype), system.shape)
    return lax.linalg.triangular_solve(lower, eye_rank, left_side=True, lower=True)


def apply_inverse(inverse, target):
    inner = jnp.einsum("hrs,hsj->hrj", inverse, target, precision=lax.Precision.HIGHEST)
    return jnp.einsum("hsr,hsj->hrj", inverse, inner, precision=lax.Precision.HIGHEST)


def make_body(runs_size, chan_size):
    runs_groups = radix_groups(runs_size, [(8, 16), (2, 4), (1,)])
    chan_bits = step_bits(chan_size, (1, 2))

    def layer(slices, spectra, loadings, mixing, halves, partner):
        run_count = slices.shape[0]
        total_runs = loadings.shape[0]
        first_run = lax.axis_index("runs") * run_count
        mine = first_run + jnp.arange(run_count, dtype=jnp.int32)
        all_runs = jnp.arange(total_runs, dtype=jnp.int32)
        matches = all_runs[None, :] == mine[:, None]
        my_halves = jnp.sum(jnp.where(matches, halves[None, :], 0), axis=1)
        my_mates = jnp.sum(jnp.where(matches, partner[None, :], 0), axis=1)
        my_loads = jnp.dot(matches.astype(jnp.float32), loadings, precision=lax.Precision.HIGHEST)
        mate_match = (all_runs[None, :] == my_mates[:, None]).astype(jnp.float32)
        mate_loads = jnp.dot(mate_match, loadings, precision=lax.Precision.HIGHEST)
        first_half = (my_halves == 0)[:, None, None]
        own_rows = jnp.where(first_half, spectra[0][None], spectra[1][None])
        own_mix = jnp.where(first_half, mixing[0][None], mixing[1][None]) * my_loads[:, None, :]
        projected = project_body(slices, own_rows, own_mix, chan_size, chan_bits)
        terms = jnp.einsum("nsr,nsj->nrj", own_mix, projected, precision=lax.Precision.HIGHEST)
        mine_member = (my_halves[:, None] == jnp.arange(2, dtype=jnp.int32)[None, :]).astype(
            jnp.float32
        )
        partial_moments = jnp.einsum(
            "nh,nrj->hrj", mine_member, terms, precision=lax.Precision.HIGHEST
        )
        member = (halves[:, None] == jnp.arange(2, dtype=jnp.int32)[None, :]).astype(jnp.float32)
        cross = jnp.einsum("kh,kr,ks->hrs", member, loadings, loadings, precision=lax.Precision.HIGHEST)
        inner_mix = jnp.einsum("hsr,hst->hrt", mixing, mixing, precision=lax.Precision.HIGHEST)
        system = inner_mix * cross
        system, partial_moments = lax.optimization_barrier((system, partial_moments))
        inverse = lower_inverse(system)
        moments_part = radix_scatter(partial_moments, "runs", runs_size, runs_groups, 2)
        spectra_part = apply_inverse(inverse, moments_part)
        new_spectra = radix_gather(spectra_part, "runs", runs_size, runs_groups, 2)
        held_rows = jnp.where(first_half, new_spectra[1][None], new_spectra[0][None])
        held_mix = jnp.where(first_half, mixing[1][None], mixing[0][None]) * mate_loads[:, None, :]
        held_projected = project_body(
            slices, held_rows.astype(jnp.bfloat16), held_mix, chan_size, chan_bits
        )
        model_part = jnp.einsum(
            "nrs,nsj->nrj", held_mix, held_rows, precision=lax.Precision.HIGHEST
        )
        return (new_spectra, held_projected - model_part)

    return layer


def solution(mesh):
    placed = (P("runs", None, "chan"), P(None, None, "chan"), P(), P(), P(), P())
    return jax.shard_map(
        make_body(mesh.shape["runs"], mesh.shape["chan"]),
        mesh=mesh,
        in_specs=placed,
        out_specs=(P(None, None, "chan"), P("runs", None, "chan")),
        check_vma=False,
    )
```

```python
import jax
import jax.numpy as jnp
from jax import lax
from jax.sharding import PartitionSpec as P

NS_STEPS = 10


def polar_scale(gram):
    eye_rank = jnp.eye(gram.shape[-1], dtype=jnp.float32)
    traces = jnp.trace(gram, axis1=1, axis2=2)
    start = eye_rank[None] / jnp.sqrt(traces + 1e-06)[:, None, None]

    def advance(step, factor):
        left = jnp.einsum("nrs,nrt->nst", factor, gram, precision=lax.Precision.HIGH)
        inner = jnp.einsum("nst,ntu->nsu", left, factor, precision=lax.Precision.HIGH)
        return 0.5 * jnp.einsum(
            "nrs,nsu->nru", factor, 3.0 * eye_rank[None] - inner, precision=lax.Precision.HIGH
        )

    return lax.fori_loop(0, NS_STEPS, advance, start)


def step_bits(size, order):
    bits = [b for b in order if b < size]
    if sorted(bits) != [1 << i for i in range(size.bit_length() - 1)]:
        bits = [1 << i for i in range(size.bit_length() - 1)]
    return bits


def xor_pairs(size, bit):
    return [(i, i ^ bit) for i in range(size)]


def halving_scatter(x, axis, size, bits, dim):
    idx = lax.axis_index(axis)
    for bit in bits:
        hi = (idx & bit) != 0
        half = x.shape[dim] // 2
        low = lax.slice_in_dim(x, 0, half, axis=dim)
        high = lax.slice_in_dim(x, half, 2 * half, axis=dim)
        send = jnp.where(hi, low, high)
        keep = jnp.where(hi, high, low)
        got = lax.ppermute(send, axis, xor_pairs(size, bit))
        x = keep + got
    return x


def doubling_gather(x, axis, size, bits, dim):
    idx = lax.axis_index(axis)
    for bit in reversed(bits):
        hi = (idx & bit) != 0
        got = lax.ppermute(x, axis, xor_pairs(size, bit))
        x = jnp.where(hi, jnp.concatenate([got, x], dim), jnp.concatenate([x, got], dim))
    return x


def digit(idx, bits):
    value = jnp.int32(0)
    for j, bit in enumerate(bits):
        value = value + ((idx & bit) != 0).astype(jnp.int32) * (1 << j)
    return value


def partner_mask(bits, offset):
    return sum(bit for j, bit in enumerate(bits) if (offset >> j) & 1)


def radix_scatter(x, axis, size, groups, dim):
    idx = lax.axis_index(axis)
    for bits in groups:
        radix = 1 << len(bits)
        width = x.shape[dim] // radix
        mine = digit(idx, bits)
        acc = lax.dynamic_slice_in_dim(x, mine * width, width, axis=dim)
        for offset in range(1, radix):
            mask = partner_mask(bits, offset)
            send = lax.dynamic_slice_in_dim(x, (mine ^ offset) * width, width, axis=dim)
            got = lax.ppermute(send, axis, xor_pairs(size, mask))
            acc = acc + got
        x = acc
    return x


def radix_gather(x, axis, size, groups, dim):
    idx = lax.axis_index(axis)
    for bits in reversed(groups):
        radix = 1 << len(bits)
        width = x.shape[dim]
        mine = digit(idx, bits)
        shape = list(x.shape)
        shape[dim] = width * radix
        out = lax.dynamic_update_slice_in_dim(jnp.zeros(shape, x.dtype), x, mine * width, axis=dim)
        for offset in range(1, radix):
            mask = partner_mask(bits, offset)
            got = lax.ppermute(x, axis, xor_pairs(size, mask))
            out = lax.dynamic_update_slice_in_dim(out, got, (mine ^ offset) * width, axis=dim)
        x = out
    return x


def radix_groups(size, groups):
    flat = sorted(bit for bits in groups for bit in bits)
    if flat != [1 << i for i in range(size.bit_length() - 1)]:
        return [(1 << i,) for i in range(size.bit_length() - 1)]
    return groups


def block_index(axis, bits):
    idx = lax.axis_index(axis)
    block = jnp.int32(0)
    for bit in bits:
        block = block * 2 + ((idx & bit) != 0).astype(jnp.int32)
    return block


def project_body(slices, rows_low, mixed, chan_size, chan_bits):
    run_count = slices.shape[0]
    scatter_bits, reduce_bits = chan_bits
    partial_basis = jnp.einsum("nrj,nij->nri", rows_low, slices, preferred_element_type=jnp.float32)
    basis = halving_scatter(partial_basis, "chan", chan_size, scatter_bits, 0)
    for bit in reduce_bits:
        got = lax.ppermute(basis, "chan", xor_pairs(chan_size, bit))
        basis = basis + got
    part = basis.shape[0]
    first = block_index("chan", scatter_bits) * part
    mixed_part = lax.dynamic_slice_in_dim(mixed, first, part, axis=0)
    scaled = jnp.einsum("nrs,nsi->nri", mixed_part, basis, precision=lax.Precision.HIGHEST)
    gram = jnp.einsum("nri,nsi->nrs", scaled, scaled, precision=lax.Precision.HIGHEST)
    factor = polar_scale(gram)
    rotated = jnp.einsum("nrs,nri->nsi", factor, scaled, precision=lax.Precision.HIGHEST).astype(
        jnp.bfloat16
    )
    rotated = doubling_gather(rotated, "chan", chan_size, scatter_bits, 0)
    del run_count
    return jnp.einsum("nsi,nij->nsj", rotated, slices, preferred_element_type=jnp.float32)


def lower_inverse(system):
    lower = jnp.linalg.cholesky(system)
    eye_rank = jnp.broadcast_to(jnp.eye(system.shape[-1], dtype=system.dtype), system.shape)
    return lax.linalg.triangular_solve(lower, eye_rank, left_side=True, lower=True)


def apply_inverse(inverse, target):
    inner = jnp.einsum("hrs,hsj->hrj", inverse, target, precision=lax.Precision.HIGHEST)
    return jnp.einsum("hsr,hsj->hrj", inverse, inner, precision=lax.Precision.HIGHEST)


def make_body(runs_size, chan_size):
    runs_groups = radix_groups(runs_size, [(8, 16), (2, 4), (1,)])
    chan_all = step_bits(chan_size, (1, 2))
    chan_bits = (chan_all[:1], chan_all[1:])

    def layer(slices, spectra, loadings, mixing, halves, partner):
        run_count = slices.shape[0]
        total_runs = loadings.shape[0]
        first_run = lax.axis_index("runs") * run_count
        mine = first_run + jnp.arange(run_count, dtype=jnp.int32)
        all_runs = jnp.arange(total_runs, dtype=jnp.int32)
        matches = all_runs[None, :] == mine[:, None]
        my_halves = jnp.sum(jnp.where(matches, halves[None, :], 0), axis=1)
        my_mates = jnp.sum(jnp.where(matches, partner[None, :], 0), axis=1)
        my_loads = jnp.dot(matches.astype(jnp.float32), loadings, precision=lax.Precision.HIGHEST)
        mate_match = (all_runs[None, :] == my_mates[:, None]).astype(jnp.float32)
        mate_loads = jnp.dot(mate_match, loadings, precision=lax.Precision.HIGHEST)
        first_half = (my_halves == 0)[:, None, None]
        own_rows = jnp.where(first_half, spectra[0][None], spectra[1][None])
        own_mix = jnp.where(first_half, mixing[0][None], mixing[1][None]) * my_loads[:, None, :]
        projected = project_body(slices, own_rows, own_mix, chan_size, chan_bits)
        mine_member = (my_halves[:, None] == jnp.arange(2, dtype=jnp.int32)[None, :]).astype(
            jnp.float32
        )
        weights = mine_member[:, :, None, None] * own_mix[:, None, :, :]
        partial_moments = jnp.einsum(
            "nhsr,nsj->hrj", weights, projected, precision=lax.Precision.HIGHEST
        )
        member = (halves[:, None] == jnp.arange(2, dtype=jnp.int32)[None, :]).astype(jnp.float32)
        cross = jnp.einsum("kh,kr,ks->hrs", member, loadings, loadings, precision=lax.Precision.HIGHEST)
        inner_mix = jnp.einsum("hsr,hst->hrt", mixing, mixing, precision=lax.Precision.HIGHEST)
        system = inner_mix * cross
        system, partial_moments = lax.optimization_barrier((system, partial_moments))
        inverse = lower_inverse(system)
        moments_part = radix_scatter(partial_moments, "runs", runs_size, runs_groups, 2)
        spectra_part = apply_inverse(inverse, moments_part)
        new_spectra = radix_gather(spectra_part, "runs", runs_size, runs_groups, 2)
        held_rows = jnp.where(first_half, new_spectra[1][None], new_spectra[0][None])
        held_mix = jnp.where(first_half, mixing[1][None], mixing[0][None]) * mate_loads[:, None, :]
        held_projected = project_body(
            slices, held_rows.astype(jnp.bfloat16), held_mix, chan_size, chan_bits
        )
        model_part = jnp.einsum(
            "nrs,nsj->nrj", held_mix, held_rows, precision=lax.Precision.HIGHEST
        )
        return (new_spectra, held_projected - model_part)

    return layer


def solution(mesh):
    placed = (P("runs", None, "chan"), P(None, None, "chan"), P(), P(), P(), P())
    return jax.shard_map(
        make_body(mesh.shape["runs"], mesh.shape["chan"]),
        mesh=mesh,
        in_specs=placed,
        out_specs=(P(None, None, "chan"), P("runs", None, "chan")),
        check_vma=False,
    )
```

```python
import jax
import jax.numpy as jnp
from jax import lax
from jax.sharding import PartitionSpec as P

NS_STEPS = 10


def polar_scale(gram):
    eye_rank = jnp.eye(gram.shape[-1], dtype=jnp.float32)
    traces = jnp.trace(gram, axis1=1, axis2=2)
    start = eye_rank[None] / jnp.sqrt(traces + 1e-06)[:, None, None]

    def advance(step, factor):
        left = jnp.einsum("nrs,nrt->nst", factor, gram, precision=lax.Precision.HIGH)
        inner = jnp.einsum("nst,ntu->nsu", left, factor, precision=lax.Precision.HIGH)
        return 0.5 * jnp.einsum(
            "nrs,nsu->nru", factor, 3.0 * eye_rank[None] - inner, precision=lax.Precision.HIGH
        )

    return lax.fori_loop(0, NS_STEPS, advance, start)


def step_bits(size, order):
    bits = [b for b in order if b < size]
    if sorted(bits) != [1 << i for i in range(size.bit_length() - 1)]:
        bits = [1 << i for i in range(size.bit_length() - 1)]
    return bits


def xor_pairs(size, bit):
    return [(i, i ^ bit) for i in range(size)]


def halving_scatter(x, axis, size, bits, dim):
    idx = lax.axis_index(axis)
    for bit in bits:
        hi = (idx & bit) != 0
        half = x.shape[dim] // 2
        low = lax.slice_in_dim(x, 0, half, axis=dim)
        high = lax.slice_in_dim(x, half, 2 * half, axis=dim)
        send = jnp.where(hi, low, high)
        keep = jnp.where(hi, high, low)
        got = lax.ppermute(send, axis, xor_pairs(size, bit))
        x = keep + got
    return x


def doubling_gather(x, axis, size, bits, dim):
    idx = lax.axis_index(axis)
    for bit in reversed(bits):
        hi = (idx & bit) != 0
        got = lax.ppermute(x, axis, xor_pairs(size, bit))
        x = jnp.where(hi, jnp.concatenate([got, x], dim), jnp.concatenate([x, got], dim))
    return x


def digit(idx, bits):
    value = jnp.int32(0)
    for j, bit in enumerate(bits):
        value = value + ((idx & bit) != 0).astype(jnp.int32) * (1 << j)
    return value


def partner_mask(bits, offset):
    return sum(bit for j, bit in enumerate(bits) if (offset >> j) & 1)


def radix_scatter(x, axis, size, groups, dim):
    idx = lax.axis_index(axis)
    for bits in groups:
        radix = 1 << len(bits)
        width = x.shape[dim] // radix
        mine = digit(idx, bits)
        acc = lax.dynamic_slice_in_dim(x, mine * width, width, axis=dim)
        for offset in range(1, radix):
            mask = partner_mask(bits, offset)
            send = lax.dynamic_slice_in_dim(x, (mine ^ offset) * width, width, axis=dim)
            got = lax.ppermute(send, axis, xor_pairs(size, mask))
            acc = acc + got
        x = acc
    return x


def radix_gather(x, axis, size, groups, dim):
    idx = lax.axis_index(axis)
    for bits in reversed(groups):
        radix = 1 << len(bits)
        width = x.shape[dim]
        mine = digit(idx, bits)
        shape = list(x.shape)
        shape[dim] = width * radix
        out = lax.dynamic_update_slice_in_dim(jnp.zeros(shape, x.dtype), x, mine * width, axis=dim)
        for offset in range(1, radix):
            mask = partner_mask(bits, offset)
            got = lax.ppermute(x, axis, xor_pairs(size, mask))
            out = lax.dynamic_update_slice_in_dim(out, got, (mine ^ offset) * width, axis=dim)
        x = out
    return x


def radix_groups(size, groups):
    flat = sorted(bit for bits in groups for bit in bits)
    if flat != [1 << i for i in range(size.bit_length() - 1)]:
        return [(1 << i,) for i in range(size.bit_length() - 1)]
    return groups


def block_index(axis, bits):
    idx = lax.axis_index(axis)
    block = jnp.int32(0)
    for bit in bits:
        block = block * 2 + ((idx & bit) != 0).astype(jnp.int32)
    return block


def project_body(slices, rows_low, mixed, chan_size, chan_bits):
    run_count = slices.shape[0]
    partial_basis = jnp.einsum("nrj,nij->nri", rows_low, slices, preferred_element_type=jnp.float32)
    basis = halving_scatter(partial_basis, "chan", chan_size, chan_bits, 0)
    part = basis.shape[0]
    first = block_index("chan", chan_bits) * part
    mixed_part = lax.dynamic_slice_in_dim(mixed, first, part, axis=0)
    scaled = jnp.einsum("nrs,nsi->nri", mixed_part, basis, precision=lax.Precision.HIGHEST)
    gram = jnp.einsum("nri,nsi->nrs", scaled, scaled, precision=lax.Precision.HIGHEST)
    factor = polar_scale(gram)
    rotated = jnp.einsum("nrs,nri->nsi", factor, scaled, precision=lax.Precision.HIGHEST).astype(
        jnp.bfloat16
    )
    rotated = doubling_gather(rotated, "chan", chan_size, chan_bits, 0)
    del run_count
    return jnp.einsum("nsi,nij->nsj", rotated, slices, preferred_element_type=jnp.float32)


def lower_inverse(system):
    lower = jnp.linalg.cholesky(system)
    eye_rank = jnp.broadcast_to(jnp.eye(system.shape[-1], dtype=system.dtype), system.shape)
    return lax.linalg.triangular_solve(lower, eye_rank, left_side=True, lower=True)


def apply_inverse(inverse, target):
    inner = jnp.einsum("hrs,hsj->hrj", inverse, target, precision=lax.Precision.HIGHEST)
    return jnp.einsum("hsr,hsj->hrj", inverse, inner, precision=lax.Precision.HIGHEST)


def make_body(runs_size, chan_size):
    runs_groups = radix_groups(runs_size, [(8, 16), (2, 4), (1,)])
    chan_bits = step_bits(chan_size, (1, 2))

    def layer(slices, spectra, loadings, mixing, halves, partner):
        run_count = slices.shape[0]
        total_runs = loadings.shape[0]
        first_run = lax.axis_index("runs") * run_count
        mine = first_run + jnp.arange(run_count, dtype=jnp.int32)
        all_runs = jnp.arange(total_runs, dtype=jnp.int32)
        matches = all_runs[None, :] == mine[:, None]
        my_halves = jnp.sum(jnp.where(matches, halves[None, :], 0), axis=1)
        my_mates = jnp.sum(jnp.where(matches, partner[None, :], 0), axis=1)
        my_loads = jnp.dot(matches.astype(jnp.float32), loadings, precision=lax.Precision.HIGHEST)
        mate_match = (all_runs[None, :] == my_mates[:, None]).astype(jnp.float32)
        mate_loads = jnp.dot(mate_match, loadings, precision=lax.Precision.HIGHEST)
        first_half = (my_halves == 0)[:, None, None]
        own_rows = jnp.where(first_half, spectra[0][None], spectra[1][None])
        own_mix = jnp.where(first_half, mixing[0][None], mixing[1][None]) * my_loads[:, None, :]
        projected = project_body(slices, own_rows, own_mix, chan_size, chan_bits)
        mine_member = (my_halves[:, None] == jnp.arange(2, dtype=jnp.int32)[None, :]).astype(
            jnp.float32
        )
        weights = mine_member[:, :, None, None] * own_mix[:, None, :, :]
        partial_moments = jnp.einsum(
            "nhsr,nsj->hrj", weights, projected, precision=lax.Precision.HIGHEST
        )
        member = (halves[:, None] == jnp.arange(2, dtype=jnp.int32)[None, :]).astype(jnp.float32)
        cross = jnp.einsum("kh,kr,ks->hrs", member, loadings, loadings, precision=lax.Precision.HIGHEST)
        inner_mix = jnp.einsum("hsr,hst->hrt", mixing, mixing, precision=lax.Precision.HIGHEST)
        system = inner_mix * cross
        system, partial_moments = lax.optimization_barrier((system, partial_moments))
        inverse = lower_inverse(system)
        moments_part = radix_scatter(partial_moments, "runs", runs_size, runs_groups, 2)
        spectra_part = apply_inverse(inverse, moments_part)
        new_spectra = radix_gather(spectra_part, "runs", runs_size, runs_groups, 2)
        held_rows = jnp.where(first_half, new_spectra[1][None], new_spectra[0][None])
        held_mix = jnp.where(first_half, mixing[1][None], mixing[0][None]) * mate_loads[:, None, :]
        held_projected = project_body(
            slices, held_rows.astype(jnp.bfloat16), held_mix, chan_size, chan_bits
        )
        model_part = jnp.einsum(
            "nrs,nsj->nrj", held_mix, held_rows, precision=lax.Precision.HIGHEST
        )
        return (new_spectra, held_projected - model_part)

    return layer


def solution(mesh):
    placed = (P("runs", None, "chan"), P(None, None, "chan"), P(), P(), P(), P())
    return jax.shard_map(
        make_body(mesh.shape["runs"], mesh.shape["chan"]),
        mesh=mesh,
        in_specs=placed,
        out_specs=(P(None, None, "chan"), P("runs", None, "chan")),
        check_vma=False,
    )
```

```python
import jax
import jax.numpy as jnp
from jax import lax
from jax.sharding import PartitionSpec as P

NS_STEPS = 10


def polar_scale(gram):
    count = gram.shape[0]
    eye_rank = jnp.eye(gram.shape[-1], dtype=jnp.float32)
    traces = jnp.trace(gram, axis1=1, axis2=2)
    scale = 1.0 / jnp.sqrt(traces + 1e-06)
    factor = eye_rank[None] * scale[:, None, None]
    inner = gram * (scale * scale)[:, None, None]
    for step in range(NS_STEPS):
        half = 0.5 * (3.0 * eye_rank[None] - inner)
        both = jnp.concatenate([factor, inner], axis=0)
        moved = jnp.einsum(
            "nrs,nsu->nru", both, jnp.concatenate([half, half], axis=0),
            precision=lax.Precision.HIGH,
        )
        factor = moved[:count]
        if step + 1 < NS_STEPS:
            inner = jnp.einsum("nrs,nsu->nru", moved[count:], half, precision=lax.Precision.HIGH)
    return factor


def step_bits(size, order):
    bits = [b for b in order if b < size]
    if sorted(bits) != [1 << i for i in range(size.bit_length() - 1)]:
        bits = [1 << i for i in range(size.bit_length() - 1)]
    return bits


def xor_pairs(size, bit):
    return [(i, i ^ bit) for i in range(size)]


def halving_scatter(x, axis, size, bits, dim):
    idx = lax.axis_index(axis)
    for bit in bits:
        hi = (idx & bit) != 0
        half = x.shape[dim] // 2
        low = lax.slice_in_dim(x, 0, half, axis=dim)
        high = lax.slice_in_dim(x, half, 2 * half, axis=dim)
        send = jnp.where(hi, low, high)
        keep = jnp.where(hi, high, low)
        got = lax.ppermute(send, axis, xor_pairs(size, bit))
        x = keep + got
    return x


def doubling_gather(x, axis, size, bits, dim):
    idx = lax.axis_index(axis)
    for bit in reversed(bits):
        hi = (idx & bit) != 0
        got = lax.ppermute(x, axis, xor_pairs(size, bit))
        x = jnp.where(hi, jnp.concatenate([got, x], dim), jnp.concatenate([x, got], dim))
    return x


def digit(idx, bits):
    value = jnp.int32(0)
    for j, bit in enumerate(bits):
        value = value + ((idx & bit) != 0).astype(jnp.int32) * (1 << j)
    return value


def partner_mask(bits, offset):
    return sum(bit for j, bit in enumerate(bits) if (offset >> j) & 1)


def radix_scatter(x, axis, size, groups, dim):
    idx = lax.axis_index(axis)
    for bits in groups:
        radix = 1 << len(bits)
        width = x.shape[dim] // radix
        mine = digit(idx, bits)
        acc = lax.dynamic_slice_in_dim(x, mine * width, width, axis=dim)
        for offset in range(1, radix):
            mask = partner_mask(bits, offset)
            send = lax.dynamic_slice_in_dim(x, (mine ^ offset) * width, width, axis=dim)
            got = lax.ppermute(send, axis, xor_pairs(size, mask))
            acc = acc + got
        x = acc
    return x


def radix_gather(x, axis, size, groups, dim):
    idx = lax.axis_index(axis)
    for bits in reversed(groups):
        radix = 1 << len(bits)
        width = x.shape[dim]
        mine = digit(idx, bits)
        shape = list(x.shape)
        shape[dim] = width * radix
        out = lax.dynamic_update_slice_in_dim(jnp.zeros(shape, x.dtype), x, mine * width, axis=dim)
        for offset in range(1, radix):
            mask = partner_mask(bits, offset)
            got = lax.ppermute(x, axis, xor_pairs(size, mask))
            out = lax.dynamic_update_slice_in_dim(out, got, (mine ^ offset) * width, axis=dim)
        x = out
    return x


def radix_groups(size, groups):
    flat = sorted(bit for bits in groups for bit in bits)
    if flat != [1 << i for i in range(size.bit_length() - 1)]:
        return [(1 << i,) for i in range(size.bit_length() - 1)]
    return groups


def block_index(axis, bits):
    idx = lax.axis_index(axis)
    block = jnp.int32(0)
    for bit in bits:
        block = block * 2 + ((idx & bit) != 0).astype(jnp.int32)
    return block


def project_body(slices, rows_low, mixed, chan_size, chan_bits):
    run_count = slices.shape[0]
    partial_basis = jnp.einsum("nrj,nij->nri", rows_low, slices, preferred_element_type=jnp.float32)
    basis = halving_scatter(partial_basis, "chan", chan_size, chan_bits, 0)
    part = basis.shape[0]
    first = block_index("chan", chan_bits) * part
    mixed_part = lax.dynamic_slice_in_dim(mixed, first, part, axis=0)
    scaled = jnp.einsum("nrs,nsi->nri", mixed_part, basis, precision=lax.Precision.HIGHEST)
    gram = jnp.einsum("nri,nsi->nrs", scaled, scaled, precision=lax.Precision.HIGHEST)
    factor = polar_scale(gram)
    rotated = jnp.einsum("nrs,nri->nsi", factor, scaled, precision=lax.Precision.HIGHEST).astype(
        jnp.bfloat16
    )
    rotated = doubling_gather(rotated, "chan", chan_size, chan_bits, 0)
    del run_count
    return jnp.einsum("nsi,nij->nsj", rotated, slices, preferred_element_type=jnp.float32)


def lower_inverse(system):
    lower = jnp.linalg.cholesky(system)
    eye_rank = jnp.broadcast_to(jnp.eye(system.shape[-1], dtype=system.dtype), system.shape)
    return lax.linalg.triangular_solve(lower, eye_rank, left_side=True, lower=True)


def apply_inverse(inverse, target):
    inner = jnp.einsum("hrs,hsj->hrj", inverse, target, precision=lax.Precision.HIGHEST)
    return jnp.einsum("hsr,hsj->hrj", inverse, inner, precision=lax.Precision.HIGHEST)


def make_body(runs_size, chan_size):
    runs_groups = radix_groups(runs_size, [(8, 16), (2, 4), (1,)])
    chan_bits = step_bits(chan_size, (1, 2))

    def layer(slices, spectra, loadings, mixing, halves, partner):
        run_count = slices.shape[0]
        total_runs = loadings.shape[0]
        first_run = lax.axis_index("runs") * run_count
        mine = first_run + jnp.arange(run_count, dtype=jnp.int32)
        all_runs = jnp.arange(total_runs, dtype=jnp.int32)
        matches = all_runs[None, :] == mine[:, None]
        my_halves = jnp.sum(jnp.where(matches, halves[None, :], 0), axis=1)
        my_mates = jnp.sum(jnp.where(matches, partner[None, :], 0), axis=1)
        my_loads = jnp.dot(matches.astype(jnp.float32), loadings, precision=lax.Precision.HIGHEST)
        mate_match = (all_runs[None, :] == my_mates[:, None]).astype(jnp.float32)
        mate_loads = jnp.dot(mate_match, loadings, precision=lax.Precision.HIGHEST)
        first_half = (my_halves == 0)[:, None, None]
        own_rows = jnp.where(first_half, spectra[0][None], spectra[1][None])
        own_mix = jnp.where(first_half, mixing[0][None], mixing[1][None]) * my_loads[:, None, :]
        projected = project_body(slices, own_rows, own_mix, chan_size, chan_bits)
        mine_member = (my_halves[:, None] == jnp.arange(2, dtype=jnp.int32)[None, :]).astype(
            jnp.float32
        )
        weights = mine_member[:, :, None, None] * own_mix[:, None, :, :]
        partial_moments = jnp.einsum(
            "nhsr,nsj->hrj", weights, projected, precision=lax.Precision.HIGHEST
        )
        member = (halves[:, None] == jnp.arange(2, dtype=jnp.int32)[None, :]).astype(jnp.float32)
        cross = jnp.einsum("kh,kr,ks->hrs", member, loadings, loadings, precision=lax.Precision.HIGHEST)
        inner_mix = jnp.einsum("hsr,hst->hrt", mixing, mixing, precision=lax.Precision.HIGHEST)
        system = inner_mix * cross
        system, partial_moments = lax.optimization_barrier((system, partial_moments))
        inverse = lower_inverse(system)
        moments_part = radix_scatter(partial_moments, "runs", runs_size, runs_groups, 2)
        spectra_part = apply_inverse(inverse, moments_part)
        new_spectra = radix_gather(spectra_part, "runs", runs_size, runs_groups, 2)
        held_rows = jnp.where(first_half, new_spectra[1][None], new_spectra[0][None])
        held_mix = jnp.where(first_half, mixing[1][None], mixing[0][None]) * mate_loads[:, None, :]
        held_projected = project_body(
            slices, held_rows.astype(jnp.bfloat16), held_mix, chan_size, chan_bits
        )
        model_part = jnp.einsum(
            "nrs,nsj->nrj", held_mix, held_rows, precision=lax.Precision.HIGHEST
        )
        return (new_spectra, held_projected - model_part)

    return layer


def solution(mesh):
    placed = (P("runs", None, "chan"), P(None, None, "chan"), P(), P(), P(), P())
    return jax.shard_map(
        make_body(mesh.shape["runs"], mesh.shape["chan"]),
        mesh=mesh,
        in_specs=placed,
        out_specs=(P(None, None, "chan"), P("runs", None, "chan")),
        check_vma=False,
    )
```

```python
import jax
import jax.numpy as jnp
from jax import lax
from jax.sharding import PartitionSpec as P

NS_STEPS = 10


def polar_scale(gram):
    count = gram.shape[0]
    eye_rank = jnp.eye(gram.shape[-1], dtype=jnp.float32)
    traces = jnp.trace(gram, axis1=1, axis2=2)
    scale = 1.0 / jnp.sqrt(traces + 1e-06)
    factor = eye_rank[None] * scale[:, None, None]
    inner = gram * (scale * scale)[:, None, None]
    for step in range(NS_STEPS):
        half = 0.5 * (3.0 * eye_rank[None] - inner)
        both = jnp.concatenate([factor, inner], axis=0)
        moved = jnp.einsum(
            "nrs,nsu->nru", both, jnp.concatenate([half, half], axis=0),
            precision=lax.Precision.HIGH,
        )
        factor = moved[:count]
        if step + 1 < NS_STEPS:
            inner = jnp.einsum("nrs,nsu->nru", moved[count:], half, precision=lax.Precision.HIGH)
    return factor


def step_bits(size, order):
    bits = [b for b in order if b < size]
    if sorted(bits) != [1 << i for i in range(size.bit_length() - 1)]:
        bits = [1 << i for i in range(size.bit_length() - 1)]
    return bits


def xor_pairs(size, bit):
    return [(i, i ^ bit) for i in range(size)]


def halving_scatter(x, axis, size, bits, dim):
    idx = lax.axis_index(axis)
    for bit in bits:
        hi = (idx & bit) != 0
        half = x.shape[dim] // 2
        low = lax.slice_in_dim(x, 0, half, axis=dim)
        high = lax.slice_in_dim(x, half, 2 * half, axis=dim)
        send = jnp.where(hi, low, high)
        keep = jnp.where(hi, high, low)
        got = lax.ppermute(send, axis, xor_pairs(size, bit))
        x = keep + got
    return x


def doubling_gather(x, axis, size, bits, dim):
    idx = lax.axis_index(axis)
    for bit in reversed(bits):
        hi = (idx & bit) != 0
        got = lax.ppermute(x, axis, xor_pairs(size, bit))
        x = jnp.where(hi, jnp.concatenate([got, x], dim), jnp.concatenate([x, got], dim))
    return x


def digit(idx, bits):
    value = jnp.int32(0)
    for j, bit in enumerate(bits):
        value = value + ((idx & bit) != 0).astype(jnp.int32) * (1 << j)
    return value


def partner_mask(bits, offset):
    return sum(bit for j, bit in enumerate(bits) if (offset >> j) & 1)


def radix_scatter(x, axis, size, groups, dim):
    idx = lax.axis_index(axis)
    for bits in groups:
        radix = 1 << len(bits)
        width = x.shape[dim] // radix
        mine = digit(idx, bits)
        acc = lax.dynamic_slice_in_dim(x, mine * width, width, axis=dim)
        for offset in range(1, radix):
            mask = partner_mask(bits, offset)
            send = lax.dynamic_slice_in_dim(x, (mine ^ offset) * width, width, axis=dim)
            got = lax.ppermute(send, axis, xor_pairs(size, mask))
            acc = acc + got
        x = acc
    return x


def radix_gather(x, axis, size, groups, dim):
    idx = lax.axis_index(axis)
    for bits in reversed(groups):
        radix = 1 << len(bits)
        width = x.shape[dim]
        mine = digit(idx, bits)
        shape = list(x.shape)
        shape[dim] = width * radix
        out = lax.dynamic_update_slice_in_dim(jnp.zeros(shape, x.dtype), x, mine * width, axis=dim)
        for offset in range(1, radix):
            mask = partner_mask(bits, offset)
            got = lax.ppermute(x, axis, xor_pairs(size, mask))
            out = lax.dynamic_update_slice_in_dim(out, got, (mine ^ offset) * width, axis=dim)
        x = out
    return x


def radix_groups(size, groups):
    flat = sorted(bit for bits in groups for bit in bits)
    if flat != [1 << i for i in range(size.bit_length() - 1)]:
        return [(1 << i,) for i in range(size.bit_length() - 1)]
    return groups


def block_index(axis, bits):
    idx = lax.axis_index(axis)
    block = jnp.int32(0)
    for bit in bits:
        block = block * 2 + ((idx & bit) != 0).astype(jnp.int32)
    return block


def project(slices, rows_low, mixed, chan_size, chan_bits, carried=None):
    return project_body(slices, rows_low, mixed, chan_size, chan_bits, carried)


def project_body(slices, rows_low, mixed, chan_size, chan_bits, carried):
    run_count = slices.shape[0]
    partial_basis = jnp.einsum("nrj,nij->nri", rows_low, slices, preferred_element_type=jnp.float32)
    if carried is not None:
        partial_basis, carried = lax.optimization_barrier((partial_basis, carried))
    basis = halving_scatter(partial_basis, "chan", chan_size, chan_bits, 0)
    part = basis.shape[0]
    first = block_index("chan", chan_bits) * part
    mixed_part = lax.dynamic_slice_in_dim(mixed, first, part, axis=0)
    scaled = jnp.einsum("nrs,nsi->nri", mixed_part, basis, precision=lax.Precision.HIGHEST)
    gram = jnp.einsum("nri,nsi->nrs", scaled, scaled, precision=lax.Precision.HIGHEST)
    factor = polar_scale(gram)
    rotated = jnp.einsum("nrs,nri->nsi", factor, scaled, precision=lax.Precision.HIGHEST).astype(
        jnp.bfloat16
    )
    rotated = doubling_gather(rotated, "chan", chan_size, chan_bits, 0)
    del run_count
    projected = jnp.einsum("nsi,nij->nsj", rotated, slices, preferred_element_type=jnp.float32)
    if carried is None:
        return projected
    return projected, carried


def lower_inverse(system):
    lower = jnp.linalg.cholesky(system)
    eye_rank = jnp.broadcast_to(jnp.eye(system.shape[-1], dtype=system.dtype), system.shape)
    return lax.linalg.triangular_solve(lower, eye_rank, left_side=True, lower=True)


def apply_inverse(inverse, target):
    inner = jnp.einsum("hrs,hsj->hrj", inverse, target, precision=lax.Precision.HIGHEST)
    return jnp.einsum("hsr,hsj->hrj", inverse, inner, precision=lax.Precision.HIGHEST)


def make_body(runs_size, chan_size):
    runs_groups = radix_groups(runs_size, [(8, 16), (2, 4), (1,)])
    chan_bits = step_bits(chan_size, (1, 2))

    def layer(slices, spectra, loadings, mixing, halves, partner):
        run_count = slices.shape[0]
        total_runs = loadings.shape[0]
        first_run = lax.axis_index("runs") * run_count
        mine = first_run + jnp.arange(run_count, dtype=jnp.int32)
        all_runs = jnp.arange(total_runs, dtype=jnp.int32)
        matches = all_runs[None, :] == mine[:, None]
        my_halves = jnp.sum(jnp.where(matches, halves[None, :], 0), axis=1)
        my_mates = jnp.sum(jnp.where(matches, partner[None, :], 0), axis=1)
        my_loads = jnp.dot(matches.astype(jnp.float32), loadings, precision=lax.Precision.HIGHEST)
        mate_match = (all_runs[None, :] == my_mates[:, None]).astype(jnp.float32)
        mate_loads = jnp.dot(mate_match, loadings, precision=lax.Precision.HIGHEST)
        first_half = (my_halves == 0)[:, None, None]
        own_rows = jnp.where(first_half, spectra[0][None], spectra[1][None])
        own_mix = jnp.where(first_half, mixing[0][None], mixing[1][None]) * my_loads[:, None, :]
        member = (halves[:, None] == jnp.arange(2, dtype=jnp.int32)[None, :]).astype(jnp.float32)
        cross = jnp.einsum("kh,kr,ks->hrs", member, loadings, loadings, precision=lax.Precision.HIGHEST)
        inner_mix = jnp.einsum("hsr,hst->hrt", mixing, mixing, precision=lax.Precision.HIGHEST)
        system = inner_mix * cross
        projected, system = project(slices, own_rows, own_mix, chan_size, chan_bits, carried=system)
        inverse = lower_inverse(system)
        mine_member = (my_halves[:, None] == jnp.arange(2, dtype=jnp.int32)[None, :]).astype(
            jnp.float32
        )
        weights = mine_member[:, :, None, None] * own_mix[:, None, :, :]
        partial_moments = jnp.einsum(
            "nhsr,nsj->hrj", weights, projected, precision=lax.Precision.HIGHEST
        )
        moments_part = radix_scatter(partial_moments, "runs", runs_size, runs_groups, 2)
        spectra_part = apply_inverse(inverse, moments_part)
        new_spectra = radix_gather(spectra_part, "runs", runs_size, runs_groups, 2)
        held_rows = jnp.where(first_half, new_spectra[1][None], new_spectra[0][None])
        held_mix = jnp.where(first_half, mixing[1][None], mixing[0][None]) * mate_loads[:, None, :]
        held_projected = project(
            slices, held_rows.astype(jnp.bfloat16), held_mix, chan_size, chan_bits
        )
        model_part = jnp.einsum(
            "nrs,nsj->nrj", held_mix, held_rows, precision=lax.Precision.HIGHEST
        )
        return (new_spectra, held_projected - model_part)

    return layer


def solution(mesh):
    placed = (P("runs", None, "chan"), P(None, None, "chan"), P(), P(), P(), P())
    return jax.shard_map(
        make_body(mesh.shape["runs"], mesh.shape["chan"]),
        mesh=mesh,
        in_specs=placed,
        out_specs=(P(None, None, "chan"), P("runs", None, "chan")),
        check_vma=False,
    )
```

```python
import jax
import jax.numpy as jnp
from jax import lax
from jax.sharding import PartitionSpec as P

NS_STEPS = 10


def polar_scale(gram):
    count = gram.shape[0]
    eye_rank = jnp.eye(gram.shape[-1], dtype=jnp.float32)
    traces = jnp.trace(gram, axis1=1, axis2=2)
    scale = 1.0 / jnp.sqrt(traces + 1e-06)
    factor = eye_rank[None] * scale[:, None, None]
    inner = gram * (scale * scale)[:, None, None]
    for step in range(NS_STEPS):
        half = 0.5 * (3.0 * eye_rank[None] - inner)
        both = jnp.concatenate([factor, inner], axis=0)
        moved = jnp.einsum(
            "nrs,nsu->nru", both, jnp.concatenate([half, half], axis=0),
            precision=lax.Precision.HIGH,
        )
        factor = moved[:count]
        if step + 1 < NS_STEPS:
            inner = jnp.einsum("nrs,nsu->nru", moved[count:], half, precision=lax.Precision.HIGH)
    return factor


def step_bits(size, order):
    bits = [b for b in order if b < size]
    if sorted(bits) != [1 << i for i in range(size.bit_length() - 1)]:
        bits = [1 << i for i in range(size.bit_length() - 1)]
    return bits


def xor_pairs(size, bit):
    return [(i, i ^ bit) for i in range(size)]


def halving_scatter(x, axis, size, bits, dim):
    idx = lax.axis_index(axis)
    for bit in bits:
        hi = (idx & bit) != 0
        half = x.shape[dim] // 2
        low = lax.slice_in_dim(x, 0, half, axis=dim)
        high = lax.slice_in_dim(x, half, 2 * half, axis=dim)
        send = jnp.where(hi, low, high)
        keep = jnp.where(hi, high, low)
        got = lax.ppermute(send, axis, xor_pairs(size, bit))
        x = keep + got
    return x


def doubling_gather(x, axis, size, bits, dim):
    idx = lax.axis_index(axis)
    for bit in reversed(bits):
        hi = (idx & bit) != 0
        got = lax.ppermute(x, axis, xor_pairs(size, bit))
        x = jnp.where(hi, jnp.concatenate([got, x], dim), jnp.concatenate([x, got], dim))
    return x


def digit(idx, bits):
    value = jnp.int32(0)
    for j, bit in enumerate(bits):
        value = value + ((idx & bit) != 0).astype(jnp.int32) * (1 << j)
    return value


def partner_mask(bits, offset):
    return sum(bit for j, bit in enumerate(bits) if (offset >> j) & 1)


def radix_scatter(x, axis, size, groups, dim):
    idx = lax.axis_index(axis)
    for bits in groups:
        radix = 1 << len(bits)
        width = x.shape[dim] // radix
        mine = digit(idx, bits)
        acc = lax.dynamic_slice_in_dim(x, mine * width, width, axis=dim)
        for offset in range(1, radix):
            mask = partner_mask(bits, offset)
            send = lax.dynamic_slice_in_dim(x, (mine ^ offset) * width, width, axis=dim)
            got = lax.ppermute(send, axis, xor_pairs(size, mask))
            acc = acc + got
        x = acc
    return x


def radix_gather(x, axis, size, groups, dim):
    idx = lax.axis_index(axis)
    for bits in reversed(groups):
        radix = 1 << len(bits)
        width = x.shape[dim]
        mine = digit(idx, bits)
        shape = list(x.shape)
        shape[dim] = width * radix
        out = lax.dynamic_update_slice_in_dim(jnp.zeros(shape, x.dtype), x, mine * width, axis=dim)
        for offset in range(1, radix):
            mask = partner_mask(bits, offset)
            got = lax.ppermute(x, axis, xor_pairs(size, mask))
            out = lax.dynamic_update_slice_in_dim(out, got, (mine ^ offset) * width, axis=dim)
        x = out
    return x


def radix_groups(size, groups):
    flat = sorted(bit for bits in groups for bit in bits)
    if flat != [1 << i for i in range(size.bit_length() - 1)]:
        return [(1 << i,) for i in range(size.bit_length() - 1)]
    return groups


def block_index(axis, bits):
    idx = lax.axis_index(axis)
    block = jnp.int32(0)
    for bit in bits:
        block = block * 2 + ((idx & bit) != 0).astype(jnp.int32)
    return block


def project(slices, rows_low, mixed, chan_size, chan_bits, carried=None):
    return project_body(slices, rows_low, mixed, chan_size, chan_bits, carried)


def project_body(slices, rows_low, mixed, chan_size, chan_bits, carried):
    run_count = slices.shape[0]
    partial_basis = jnp.einsum("nrj,nij->nri", rows_low, slices, preferred_element_type=jnp.float32)
    if carried is not None:
        carried = lax.optimization_barrier((partial_basis, carried))[1]
    basis = halving_scatter(partial_basis, "chan", chan_size, chan_bits, 0)
    part = basis.shape[0]
    first = block_index("chan", chan_bits) * part
    mixed_part = lax.dynamic_slice_in_dim(mixed, first, part, axis=0)
    scaled = jnp.einsum("nrs,nsi->nri", mixed_part, basis, precision=lax.Precision.HIGHEST)
    gram = jnp.einsum("nri,nsi->nrs", scaled, scaled, precision=lax.Precision.HIGHEST)
    factor = polar_scale(gram)
    rotated = jnp.einsum("nrs,nri->nsi", factor, scaled, precision=lax.Precision.HIGHEST).astype(
        jnp.bfloat16
    )
    rotated = doubling_gather(rotated, "chan", chan_size, chan_bits, 0)
    del run_count
    projected = jnp.einsum("nsi,nij->nsj", rotated, slices, preferred_element_type=jnp.float32)
    if carried is None:
        return projected
    return projected, carried


def lower_inverse(system):
    lower = jnp.linalg.cholesky(system)
    eye_rank = jnp.broadcast_to(jnp.eye(system.shape[-1], dtype=system.dtype), system.shape)
    return lax.linalg.triangular_solve(lower, eye_rank, left_side=True, lower=True)


def apply_inverse(inverse, target):
    inner = jnp.einsum("hrs,hsj->hrj", inverse, target, precision=lax.Precision.HIGHEST)
    return jnp.einsum("hsr,hsj->hrj", inverse, inner, precision=lax.Precision.HIGHEST)


def make_body(runs_size, chan_size):
    runs_groups = radix_groups(runs_size, [(8, 16), (2, 4), (1,)])
    chan_bits = step_bits(chan_size, (1, 2))

    def layer(slices, spectra, loadings, mixing, halves, partner):
        run_count = slices.shape[0]
        total_runs = loadings.shape[0]
        first_run = lax.axis_index("runs") * run_count
        mine = first_run + jnp.arange(run_count, dtype=jnp.int32)
        all_runs = jnp.arange(total_runs, dtype=jnp.int32)
        matches = all_runs[None, :] == mine[:, None]
        my_halves = jnp.sum(jnp.where(matches, halves[None, :], 0), axis=1)
        my_mates = jnp.sum(jnp.where(matches, partner[None, :], 0), axis=1)
        my_loads = jnp.dot(matches.astype(jnp.float32), loadings, precision=lax.Precision.HIGHEST)
        mate_match = (all_runs[None, :] == my_mates[:, None]).astype(jnp.float32)
        mate_loads = jnp.dot(mate_match, loadings, precision=lax.Precision.HIGHEST)
        first_half = (my_halves == 0)[:, None, None]
        own_rows = jnp.where(first_half, spectra[0][None], spectra[1][None])
        own_mix = jnp.where(first_half, mixing[0][None], mixing[1][None]) * my_loads[:, None, :]
        member = (halves[:, None] == jnp.arange(2, dtype=jnp.int32)[None, :]).astype(jnp.float32)
        cross = jnp.einsum(
            "kh,kr,ks->hrs", member, loadings, loadings, precision=lax.Precision.HIGHEST
        )
        inner_mix = jnp.einsum(
            "hsr,hst->hrt", mixing, mixing, precision=lax.Precision.HIGHEST
        )
        system = inner_mix * cross
        projected, system = project(slices, own_rows, own_mix, chan_size, chan_bits, carried=system)
        inverse = lower_inverse(system)
        mine_member = (my_halves[:, None] == jnp.arange(2, dtype=jnp.int32)[None, :]).astype(
            jnp.float32
        )
        weights = mine_member[:, :, None, None] * own_mix[:, None, :, :]
        partial_moments = jnp.einsum(
            "nhsr,nsj->hrj", weights, projected, precision=lax.Precision.HIGHEST
        )
        moments_part = radix_scatter(partial_moments, "runs", runs_size, runs_groups, 2)
        spectra_part = apply_inverse(inverse, moments_part)
        new_spectra = radix_gather(spectra_part, "runs", runs_size, runs_groups, 2)
        held_rows = jnp.where(first_half, new_spectra[1][None], new_spectra[0][None])
        held_mix = jnp.where(first_half, mixing[1][None], mixing[0][None]) * mate_loads[:, None, :]
        held_projected = project(
            slices, held_rows.astype(jnp.bfloat16), held_mix, chan_size, chan_bits
        )
        model_part = jnp.einsum(
            "nrs,nsj->nrj", held_mix, held_rows, precision=lax.Precision.HIGHEST
        )
        return (new_spectra, held_projected - model_part)

    return layer


def solution(mesh):
    placed = (P("runs", None, "chan"), P(None, None, "chan"), P(), P(), P(), P())
    return jax.shard_map(
        make_body(mesh.shape["runs"], mesh.shape["chan"]),
        mesh=mesh,
        in_specs=placed,
        out_specs=(P(None, None, "chan"), P("runs", None, "chan")),
        check_vma=False,
    )
```

```python
import jax
import jax.numpy as jnp
from jax import lax
from jax.sharding import PartitionSpec as P

NS_STEPS = 10


def polar_scale(gram):
    count = gram.shape[0]
    eye_rank = jnp.eye(gram.shape[-1], dtype=jnp.float32)
    traces = jnp.trace(gram, axis1=1, axis2=2)
    scale = 1.0 / jnp.sqrt(traces + 1e-06)
    factor = eye_rank[None] * scale[:, None, None]
    inner = gram * (scale * scale)[:, None, None]
    for step in range(NS_STEPS):
        half = 0.5 * (3.0 * eye_rank[None] - inner)
        both = jnp.concatenate([factor, inner], axis=0)
        moved = jnp.einsum(
            "nrs,nsu->nru", both, jnp.concatenate([half, half], axis=0),
            precision=lax.Precision.HIGH,
        )
        factor = moved[:count]
        if step + 1 < NS_STEPS:
            inner = jnp.einsum("nrs,nsu->nru", moved[count:], half, precision=lax.Precision.HIGH)
    return factor


def step_bits(size, order):
    bits = [b for b in order if b < size]
    if sorted(bits) != [1 << i for i in range(size.bit_length() - 1)]:
        bits = [1 << i for i in range(size.bit_length() - 1)]
    return bits


def xor_pairs(size, bit):
    return [(i, i ^ bit) for i in range(size)]


def halving_scatter(x, axis, size, bits, dim):
    idx = lax.axis_index(axis)
    for bit in bits:
        hi = (idx & bit) != 0
        half = x.shape[dim] // 2
        low = lax.slice_in_dim(x, 0, half, axis=dim)
        high = lax.slice_in_dim(x, half, 2 * half, axis=dim)
        send = jnp.where(hi, low, high)
        keep = jnp.where(hi, high, low)
        got = lax.ppermute(send, axis, xor_pairs(size, bit))
        x = keep + got
    return x


def doubling_gather(x, axis, size, bits, dim):
    idx = lax.axis_index(axis)
    for bit in reversed(bits):
        hi = (idx & bit) != 0
        got = lax.ppermute(x, axis, xor_pairs(size, bit))
        x = jnp.where(hi, jnp.concatenate([got, x], dim), jnp.concatenate([x, got], dim))
    return x


def digit(idx, bits):
    value = jnp.int32(0)
    for j, bit in enumerate(bits):
        value = value + ((idx & bit) != 0).astype(jnp.int32) * (1 << j)
    return value


def partner_mask(bits, offset):
    return sum(bit for j, bit in enumerate(bits) if (offset >> j) & 1)


def radix_scatter(x, axis, size, groups, dim):
    idx = lax.axis_index(axis)
    for bits in groups:
        radix = 1 << len(bits)
        width = x.shape[dim] // radix
        mine = digit(idx, bits)
        acc = lax.dynamic_slice_in_dim(x, mine * width, width, axis=dim)
        for offset in range(1, radix):
            mask = partner_mask(bits, offset)
            send = lax.dynamic_slice_in_dim(x, (mine ^ offset) * width, width, axis=dim)
            got = lax.ppermute(send, axis, xor_pairs(size, mask))
            acc = acc + got
        x = acc
    return x


def radix_gather(x, axis, size, groups, dim):
    idx = lax.axis_index(axis)
    for bits in reversed(groups):
        radix = 1 << len(bits)
        width = x.shape[dim]
        mine = digit(idx, bits)
        shape = list(x.shape)
        shape[dim] = width * radix
        out = lax.dynamic_update_slice_in_dim(jnp.zeros(shape, x.dtype), x, mine * width, axis=dim)
        for offset in range(1, radix):
            mask = partner_mask(bits, offset)
            got = lax.ppermute(x, axis, xor_pairs(size, mask))
            out = lax.dynamic_update_slice_in_dim(out, got, (mine ^ offset) * width, axis=dim)
        x = out
    return x


def radix_groups(size, groups):
    flat = sorted(bit for bits in groups for bit in bits)
    if flat != [1 << i for i in range(size.bit_length() - 1)]:
        return [(1 << i,) for i in range(size.bit_length() - 1)]
    return groups


def block_index(axis, bits):
    idx = lax.axis_index(axis)
    block = jnp.int32(0)
    for bit in bits:
        block = block * 2 + ((idx & bit) != 0).astype(jnp.int32)
    return block


def project(slices, rows_low, mixed, chan_size, chan_bits, carried=None):
    return project_body(slices, rows_low, mixed, chan_size, chan_bits, carried)


def project_body(slices, rows_low, mixed, chan_size, chan_bits, carried):
    run_count = slices.shape[0]
    partial_basis = jnp.einsum("nrj,nij->nri", rows_low, slices, preferred_element_type=jnp.float32)
    if carried is not None:
        carried = lax.optimization_barrier((partial_basis, carried))[1]
    basis = halving_scatter(partial_basis, "chan", chan_size, chan_bits, 0)
    part = basis.shape[0]
    first = block_index("chan", chan_bits) * part
    mixed_part = lax.dynamic_slice_in_dim(mixed, first, part, axis=0)
    scaled = jnp.einsum("nrs,nsi->nri", mixed_part, basis, precision=lax.Precision.HIGHEST)
    gram = jnp.einsum("nri,nsi->nrs", scaled, scaled, precision=lax.Precision.HIGHEST)
    factor = polar_scale(gram)
    rotated = jnp.einsum("nrs,nri->nsi", factor, scaled, precision=lax.Precision.HIGHEST).astype(
        jnp.bfloat16
    )
    rotated = doubling_gather(rotated, "chan", chan_size, chan_bits, 0)
    del run_count
    projected = jnp.einsum("nsi,nij->nsj", rotated, slices, preferred_element_type=jnp.float32)
    if carried is None:
        return projected
    return projected, carried


def lower_inverse(system):
    lower = jnp.linalg.cholesky(system)
    eye_rank = jnp.broadcast_to(jnp.eye(system.shape[-1], dtype=system.dtype), system.shape)
    return lax.linalg.triangular_solve(lower, eye_rank, left_side=True, lower=True)


def apply_inverse(inverse, target):
    inner = jnp.einsum("hrs,hsj->hrj", inverse, target, precision=lax.Precision.HIGHEST)
    return jnp.einsum("hsr,hsj->hrj", inverse, inner, precision=lax.Precision.HIGHEST)


def make_body(runs_size, chan_size):
    runs_groups = radix_groups(runs_size, [(8, 16), (2, 4), (1,)])
    chan_bits = step_bits(chan_size, (1, 2))

    def layer(slices, spectra, loadings, mixing, halves, partner):
        run_count = slices.shape[0]
        total_runs = loadings.shape[0]
        first_run = lax.axis_index("runs") * run_count
        mine = first_run + jnp.arange(run_count, dtype=jnp.int32)
        all_runs = jnp.arange(total_runs, dtype=jnp.int32)
        matches = all_runs[None, :] == mine[:, None]
        my_halves = jnp.sum(jnp.where(matches, halves[None, :], 0), axis=1)
        my_mates = jnp.sum(jnp.where(matches, partner[None, :], 0), axis=1)
        my_loads = jnp.dot(matches.astype(jnp.float32), loadings, precision=lax.Precision.HIGHEST)
        mate_match = (all_runs[None, :] == my_mates[:, None]).astype(jnp.float32)
        mate_loads = jnp.dot(mate_match, loadings, precision=lax.Precision.HIGHEST)
        first_half = (my_halves == 0)[:, None, None]
        own_rows = jnp.where(first_half, spectra[0][None], spectra[1][None])
        own_mix = jnp.where(first_half, mixing[0][None], mixing[1][None]) * my_loads[:, None, :]
        member = (halves[:, None] == jnp.arange(2, dtype=jnp.int32)[None, :]).astype(jnp.float32)
        cross = jnp.einsum(
            "kh,kr,ks->hrs", member, loadings, loadings, precision=lax.Precision.HIGHEST
        )
        inner_mix = jnp.einsum(
            "hsr,hst->hrt", mixing, mixing, precision=lax.Precision.HIGHEST
        )
        system = inner_mix * cross
        projected, system = project(slices, own_rows, own_mix, chan_size, chan_bits, carried=system)
        inverse = lower_inverse(system)
        mine_member = (my_halves[:, None] == jnp.arange(2, dtype=jnp.int32)[None, :]).astype(
            jnp.float32
        )
        weights = mine_member[:, :, None, None] * own_mix[:, None, :, :]
        partial_moments = jnp.einsum(
            "nhsr,nsj->hrj", weights, projected, precision=lax.Precision.HIGH
        )
        moments_part = radix_scatter(partial_moments, "runs", runs_size, runs_groups, 2)
        spectra_part = apply_inverse(inverse, moments_part)
        new_spectra = radix_gather(spectra_part, "runs", runs_size, runs_groups, 2)
        held_rows = jnp.where(first_half, new_spectra[1][None], new_spectra[0][None])
        held_mix = jnp.where(first_half, mixing[1][None], mixing[0][None]) * mate_loads[:, None, :]
        held_projected = project(
            slices, held_rows.astype(jnp.bfloat16), held_mix, chan_size, chan_bits
        )
        model_part = jnp.einsum("nrs,nsj->nrj", held_mix, held_rows, precision=lax.Precision.HIGH)
        return (new_spectra, held_projected - model_part)

    return layer


def solution(mesh):
    placed = (P("runs", None, "chan"), P(None, None, "chan"), P(), P(), P(), P())
    return jax.shard_map(
        make_body(mesh.shape["runs"], mesh.shape["chan"]),
        mesh=mesh,
        in_specs=placed,
        out_specs=(P(None, None, "chan"), P("runs", None, "chan")),
        check_vma=False,
    )
```

```python
import jax
import jax.numpy as jnp
from jax import lax
from jax.sharding import PartitionSpec as P

NS_STEPS = 10


def polar_scale(gram):
    count = gram.shape[0]
    eye_rank = jnp.eye(gram.shape[-1], dtype=jnp.float32)
    traces = jnp.trace(gram, axis1=1, axis2=2)
    scale = 1.0 / jnp.sqrt(traces + 1e-06)
    factor = eye_rank[None] * scale[:, None, None]
    inner = gram * (scale * scale)[:, None, None]
    for step in range(NS_STEPS):
        half = 0.5 * (3.0 * eye_rank[None] - inner)
        both = jnp.concatenate([factor, inner], axis=0)
        moved = jnp.einsum(
            "nrs,nsu->nru", both, jnp.concatenate([half, half], axis=0),
            precision=lax.Precision.HIGH,
        )
        factor = moved[:count]
        if step + 1 < NS_STEPS:
            inner = jnp.einsum("nrs,nsu->nru", moved[count:], half, precision=lax.Precision.HIGH)
    return factor


def step_bits(size, order):
    bits = [b for b in order if b < size]
    if sorted(bits) != [1 << i for i in range(size.bit_length() - 1)]:
        bits = [1 << i for i in range(size.bit_length() - 1)]
    return bits


def xor_pairs(size, bit):
    return [(i, i ^ bit) for i in range(size)]


def halving_scatter(x, axis, size, bits, dim):
    idx = lax.axis_index(axis)
    for bit in bits:
        hi = (idx & bit) != 0
        half = x.shape[dim] // 2
        low = lax.slice_in_dim(x, 0, half, axis=dim)
        high = lax.slice_in_dim(x, half, 2 * half, axis=dim)
        send = jnp.where(hi, low, high)
        keep = jnp.where(hi, high, low)
        got = lax.ppermute(send, axis, xor_pairs(size, bit))
        x = keep + got
    return x


def doubling_gather(x, axis, size, bits, dim):
    idx = lax.axis_index(axis)
    for bit in reversed(bits):
        hi = (idx & bit) != 0
        got = lax.ppermute(x, axis, xor_pairs(size, bit))
        x = jnp.where(hi, jnp.concatenate([got, x], dim), jnp.concatenate([x, got], dim))
    return x


def digit(idx, bits):
    value = jnp.int32(0)
    for j, bit in enumerate(bits):
        value = value + ((idx & bit) != 0).astype(jnp.int32) * (1 << j)
    return value


def partner_mask(bits, offset):
    return sum(bit for j, bit in enumerate(bits) if (offset >> j) & 1)


def radix_scatter(x, axis, size, groups, dim):
    idx = lax.axis_index(axis)
    for bits in groups:
        radix = 1 << len(bits)
        width = x.shape[dim] // radix
        mine = digit(idx, bits)
        acc = lax.dynamic_slice_in_dim(x, mine * width, width, axis=dim)
        for offset in range(1, radix):
            mask = partner_mask(bits, offset)
            send = lax.dynamic_slice_in_dim(x, (mine ^ offset) * width, width, axis=dim)
            got = lax.ppermute(send, axis, xor_pairs(size, mask))
            acc = acc + got
        x = acc
    return x


def radix_gather(x, axis, size, groups, dim):
    idx = lax.axis_index(axis)
    for bits in reversed(groups):
        radix = 1 << len(bits)
        width = x.shape[dim]
        mine = digit(idx, bits)
        shape = list(x.shape)
        shape[dim] = width * radix
        out = lax.dynamic_update_slice_in_dim(jnp.zeros(shape, x.dtype), x, mine * width, axis=dim)
        for offset in range(1, radix):
            mask = partner_mask(bits, offset)
            got = lax.ppermute(x, axis, xor_pairs(size, mask))
            out = lax.dynamic_update_slice_in_dim(out, got, (mine ^ offset) * width, axis=dim)
        x = out
    return x


def radix_groups(size, groups):
    flat = sorted(bit for bits in groups for bit in bits)
    if flat != [1 << i for i in range(size.bit_length() - 1)]:
        return [(1 << i,) for i in range(size.bit_length() - 1)]
    return groups


def block_index(axis, bits):
    idx = lax.axis_index(axis)
    block = jnp.int32(0)
    for bit in bits:
        block = block * 2 + ((idx & bit) != 0).astype(jnp.int32)
    return block


def project(slices, rows_low, mixed, chan_size, chan_bits, carried=None):
    return project_body(slices, rows_low, mixed, chan_size, chan_bits, carried)


def project_body(slices, rows_low, mixed, chan_size, chan_bits, carried):
    run_count = slices.shape[0]
    rows_both, pick = rows_low
    partial_both = jnp.einsum(
        "hrj,nij->nhri", rows_both, slices, preferred_element_type=jnp.float32
    )
    partial_basis = jnp.where((pick == 0)[:, None, None], partial_both[:, 0], partial_both[:, 1])
    if carried is not None:
        carried = lax.optimization_barrier((partial_basis, carried))[1]
    basis = halving_scatter(partial_basis, "chan", chan_size, chan_bits, 0)
    part = basis.shape[0]
    first = block_index("chan", chan_bits) * part
    mixed_part = lax.dynamic_slice_in_dim(mixed, first, part, axis=0)
    scaled = jnp.einsum("nrs,nsi->nri", mixed_part, basis, precision=lax.Precision.HIGHEST)
    gram = jnp.einsum("nri,nsi->nrs", scaled, scaled, precision=lax.Precision.HIGHEST)
    factor = polar_scale(gram)
    rotated = jnp.einsum("nrs,nri->nsi", factor, scaled, precision=lax.Precision.HIGHEST).astype(
        jnp.bfloat16
    )
    rotated = doubling_gather(rotated, "chan", chan_size, chan_bits, 0)
    del run_count
    projected = jnp.einsum("nsi,nij->nsj", rotated, slices, preferred_element_type=jnp.float32)
    if carried is None:
        return projected
    return projected, carried


def lower_inverse(system):
    lower = jnp.linalg.cholesky(system)
    eye_rank = jnp.broadcast_to(jnp.eye(system.shape[-1], dtype=system.dtype), system.shape)
    return lax.linalg.triangular_solve(lower, eye_rank, left_side=True, lower=True)


def apply_inverse(inverse, target):
    inner = jnp.einsum("hrs,hsj->hrj", inverse, target, precision=lax.Precision.HIGHEST)
    return jnp.einsum("hsr,hsj->hrj", inverse, inner, precision=lax.Precision.HIGHEST)


def make_body(runs_size, chan_size):
    runs_groups = radix_groups(runs_size, [(8, 16), (2, 4), (1,)])
    chan_bits = step_bits(chan_size, (1, 2))

    def layer(slices, spectra, loadings, mixing, halves, partner):
        run_count = slices.shape[0]
        total_runs = loadings.shape[0]
        first_run = lax.axis_index("runs") * run_count
        mine = first_run + jnp.arange(run_count, dtype=jnp.int32)
        all_runs = jnp.arange(total_runs, dtype=jnp.int32)
        matches = all_runs[None, :] == mine[:, None]
        my_halves = jnp.sum(jnp.where(matches, halves[None, :], 0), axis=1)
        my_mates = jnp.sum(jnp.where(matches, partner[None, :], 0), axis=1)
        my_loads = jnp.dot(matches.astype(jnp.float32), loadings, precision=lax.Precision.HIGHEST)
        mate_match = (all_runs[None, :] == my_mates[:, None]).astype(jnp.float32)
        mate_loads = jnp.dot(mate_match, loadings, precision=lax.Precision.HIGHEST)
        first_half = (my_halves == 0)[:, None, None]
        own_mix = jnp.where(first_half, mixing[0][None], mixing[1][None]) * my_loads[:, None, :]
        member = (halves[:, None] == jnp.arange(2, dtype=jnp.int32)[None, :]).astype(jnp.float32)
        cross = jnp.einsum(
            "kh,kr,ks->hrs", member, loadings, loadings, precision=lax.Precision.HIGHEST
        )
        inner_mix = jnp.einsum(
            "hsr,hst->hrt", mixing, mixing, precision=lax.Precision.HIGHEST
        )
        system = inner_mix * cross
        projected, system = project(
            slices, (spectra, my_halves), own_mix, chan_size, chan_bits, carried=system
        )
        inverse = lower_inverse(system)
        mine_member = (my_halves[:, None] == jnp.arange(2, dtype=jnp.int32)[None, :]).astype(
            jnp.float32
        )
        weights = mine_member[:, :, None, None] * own_mix[:, None, :, :]
        partial_moments = jnp.einsum(
            "nhsr,nsj->hrj", weights, projected, precision=lax.Precision.HIGHEST
        )
        moments_part = radix_scatter(partial_moments, "runs", runs_size, runs_groups, 2)
        spectra_part = apply_inverse(inverse, moments_part)
        new_spectra = radix_gather(spectra_part, "runs", runs_size, runs_groups, 2)
        held_rows = jnp.where(first_half, new_spectra[1][None], new_spectra[0][None])
        held_mix = jnp.where(first_half, mixing[1][None], mixing[0][None]) * mate_loads[:, None, :]
        held_projected = project(
            slices, (new_spectra.astype(jnp.bfloat16), 1 - my_halves), held_mix, chan_size,
            chan_bits,
        )
        model_part = jnp.einsum(
            "nrs,nsj->nrj", held_mix, held_rows, precision=lax.Precision.HIGHEST
        )
        return (new_spectra, held_projected - model_part)

    return layer


def solution(mesh):
    placed = (P("runs", None, "chan"), P(None, None, "chan"), P(), P(), P(), P())
    return jax.shard_map(
        make_body(mesh.shape["runs"], mesh.shape["chan"]),
        mesh=mesh,
        in_specs=placed,
        out_specs=(P(None, None, "chan"), P("runs", None, "chan")),
        check_vma=False,
    )
```

```python
import jax
import jax.numpy as jnp
from jax import lax
from jax.sharding import PartitionSpec as P

NS_STEPS = 10


def polar_scale(gram):
    count = gram.shape[0]
    eye_rank = jnp.eye(gram.shape[-1], dtype=jnp.float32)
    traces = jnp.trace(gram, axis1=1, axis2=2)
    scale = 1.0 / jnp.sqrt(traces + 1e-06)
    factor = eye_rank[None] * scale[:, None, None]
    inner = gram * (scale * scale)[:, None, None]
    for step in range(NS_STEPS):
        half = 0.5 * (3.0 * eye_rank[None] - inner)
        both = jnp.concatenate([factor, inner], axis=0)
        moved = jnp.einsum(
            "nrs,nsu->nru", both, jnp.concatenate([half, half], axis=0),
            precision=lax.Precision.HIGH,
        )
        factor = moved[:count]
        if step + 1 < NS_STEPS:
            inner = jnp.einsum("nrs,nsu->nru", moved[count:], half, precision=lax.Precision.HIGH)
    return factor


def step_bits(size, order):
    bits = [b for b in order if b < size]
    if sorted(bits) != [1 << i for i in range(size.bit_length() - 1)]:
        bits = [1 << i for i in range(size.bit_length() - 1)]
    return bits


def xor_pairs(size, bit):
    return [(i, i ^ bit) for i in range(size)]


def halving_scatter(x, axis, size, bits, dim):
    idx = lax.axis_index(axis)
    for bit in bits:
        hi = (idx & bit) != 0
        half = x.shape[dim] // 2
        low = lax.slice_in_dim(x, 0, half, axis=dim)
        high = lax.slice_in_dim(x, half, 2 * half, axis=dim)
        send = jnp.where(hi, low, high)
        keep = jnp.where(hi, high, low)
        got = lax.ppermute(send, axis, xor_pairs(size, bit))
        x = keep + got
    return x


def doubling_gather(x, axis, size, bits, dim):
    idx = lax.axis_index(axis)
    for bit in reversed(bits):
        hi = (idx & bit) != 0
        got = lax.ppermute(x, axis, xor_pairs(size, bit))
        x = jnp.where(hi, jnp.concatenate([got, x], dim), jnp.concatenate([x, got], dim))
    return x


def digit(idx, bits):
    value = jnp.int32(0)
    for j, bit in enumerate(bits):
        value = value + ((idx & bit) != 0).astype(jnp.int32) * (1 << j)
    return value


def partner_mask(bits, offset):
    return sum(bit for j, bit in enumerate(bits) if (offset >> j) & 1)


def radix_scatter(x, axis, size, groups, dim):
    idx = lax.axis_index(axis)
    for bits in groups:
        radix = 1 << len(bits)
        width = x.shape[dim] // radix
        mine = digit(idx, bits)
        acc = lax.dynamic_slice_in_dim(x, mine * width, width, axis=dim)
        for offset in range(1, radix):
            mask = partner_mask(bits, offset)
            send = lax.dynamic_slice_in_dim(x, (mine ^ offset) * width, width, axis=dim)
            got = lax.ppermute(send, axis, xor_pairs(size, mask))
            acc = acc + got
        x = acc
    return x


def radix_gather(x, axis, size, groups, dim):
    idx = lax.axis_index(axis)
    for bits in reversed(groups):
        radix = 1 << len(bits)
        width = x.shape[dim]
        mine = digit(idx, bits)
        shape = list(x.shape)
        shape[dim] = width * radix
        out = lax.dynamic_update_slice_in_dim(jnp.zeros(shape, x.dtype), x, mine * width, axis=dim)
        for offset in range(1, radix):
            mask = partner_mask(bits, offset)
            got = lax.ppermute(x, axis, xor_pairs(size, mask))
            out = lax.dynamic_update_slice_in_dim(out, got, (mine ^ offset) * width, axis=dim)
        x = out
    return x


def radix_groups(size, groups):
    flat = sorted(bit for bits in groups for bit in bits)
    if flat != [1 << i for i in range(size.bit_length() - 1)]:
        return [(1 << i,) for i in range(size.bit_length() - 1)]
    return groups


def block_index(axis, bits):
    idx = lax.axis_index(axis)
    block = jnp.int32(0)
    for bit in bits:
        block = block * 2 + ((idx & bit) != 0).astype(jnp.int32)
    return block


def project(slices, rows_low, mixed, chan_size, chan_bits, carried=None):
    return project_body(slices, rows_low, mixed, chan_size, chan_bits, carried)


def project_body(slices, rows_low, mixed, chan_size, chan_bits, carried):
    run_count = slices.shape[0]
    rows_both, pick = rows_low
    partial_both = jnp.einsum(
        "hrj,nij->nhri", rows_both, slices, preferred_element_type=jnp.float32
    )
    partial_basis = jnp.where((pick == 0)[:, None, None], partial_both[:, 0], partial_both[:, 1])
    if carried is not None:
        carried = lax.optimization_barrier((partial_basis, carried))[1]
    basis = halving_scatter(partial_basis, "chan", chan_size, chan_bits, 0)
    part = basis.shape[0]
    first = block_index("chan", chan_bits) * part
    mixed_part = lax.dynamic_slice_in_dim(mixed, first, part, axis=0)
    scaled = jnp.einsum("nrs,nsi->nri", mixed_part, basis, precision=lax.Precision.HIGHEST)
    gram = jnp.einsum("nri,nsi->nrs", scaled, scaled, precision=lax.Precision.HIGHEST)
    factor = polar_scale(gram)
    rotated = jnp.einsum("nrs,nri->nsi", factor, scaled, precision=lax.Precision.HIGHEST).astype(
        jnp.bfloat16
    )
    rotated = doubling_gather(rotated, "chan", chan_size, chan_bits, 0)
    del run_count
    projected = jnp.einsum("nsi,nij->nsj", rotated, slices, preferred_element_type=jnp.float32)
    if carried is None:
        return projected
    return projected, carried


def lower_inverse(system):
    lower = jnp.linalg.cholesky(system)
    eye_rank = jnp.broadcast_to(jnp.eye(system.shape[-1], dtype=system.dtype), system.shape)
    return lax.linalg.triangular_solve(lower, eye_rank, left_side=True, lower=True)


def apply_inverse(inverse, target):
    inner = jnp.einsum("hrs,hsj->hrj", inverse, target, precision=lax.Precision.HIGHEST)
    return jnp.einsum("hsr,hsj->hrj", inverse, inner, precision=lax.Precision.HIGHEST)


def make_body(runs_size, chan_size):
    runs_groups = radix_groups(runs_size, [(8, 16), (2, 4), (1,)])
    chan_bits = step_bits(chan_size, (1, 2))

    def layer(slices, spectra, loadings, mixing, halves, partner):
        run_count = slices.shape[0]
        total_runs = loadings.shape[0]
        first_run = lax.axis_index("runs") * run_count
        del total_runs
        my_halves = lax.dynamic_slice_in_dim(halves, first_run, run_count)
        my_mates = lax.dynamic_slice_in_dim(partner, first_run, run_count)
        my_loads = lax.dynamic_slice_in_dim(loadings, first_run, run_count, axis=0)
        mate_loads = jnp.take(loadings, my_mates, axis=0, mode="clip")
        first_half = (my_halves == 0)[:, None, None]
        own_mix = jnp.where(first_half, mixing[0][None], mixing[1][None]) * my_loads[:, None, :]
        member = (halves[:, None] == jnp.arange(2, dtype=jnp.int32)[None, :]).astype(jnp.float32)
        cross = jnp.einsum(
            "kh,kr,ks->hrs", member, loadings, loadings, precision=lax.Precision.HIGHEST
        )
        inner_mix = jnp.einsum(
            "hsr,hst->hrt", mixing, mixing, precision=lax.Precision.HIGHEST
        )
        system = inner_mix * cross
        projected, system = project(
            slices, (spectra, my_halves), own_mix, chan_size, chan_bits, carried=system
        )
        inverse = lower_inverse(system)
        mine_member = (my_halves[:, None] == jnp.arange(2, dtype=jnp.int32)[None, :]).astype(
            jnp.float32
        )
        weights = mine_member[:, :, None, None] * own_mix[:, None, :, :]
        partial_moments = jnp.einsum(
            "nhsr,nsj->hrj", weights, projected, precision=lax.Precision.HIGHEST
        )
        moments_part = radix_scatter(partial_moments, "runs", runs_size, runs_groups, 2)
        spectra_part = apply_inverse(inverse, moments_part)
        new_spectra = radix_gather(spectra_part, "runs", runs_size, runs_groups, 2)
        held_rows = jnp.where(first_half, new_spectra[1][None], new_spectra[0][None])
        held_mix = jnp.where(first_half, mixing[1][None], mixing[0][None]) * mate_loads[:, None, :]
        held_projected = project(
            slices, (new_spectra.astype(jnp.bfloat16), 1 - my_halves), held_mix, chan_size,
            chan_bits,
        )
        model_part = jnp.einsum(
            "nrs,nsj->nrj", held_mix, held_rows, precision=lax.Precision.HIGHEST
        )
        return (new_spectra, held_projected - model_part)

    return layer


def solution(mesh):
    placed = (P("runs", None, "chan"), P(None, None, "chan"), P(), P(), P(), P())
    return jax.shard_map(
        make_body(mesh.shape["runs"], mesh.shape["chan"]),
        mesh=mesh,
        in_specs=placed,
        out_specs=(P(None, None, "chan"), P("runs", None, "chan")),
        check_vma=False,
    )
```
